128 devices in a mesh: ens: 8 (over y, core), trc: 16 (over z, x).
Axes of the slice: x: 4, y: 4, z: 4, core: 2. Of those that a mesh axis runs over, the one named last changes fastest.
Arguments:
- tracer_state: bfloat16 [3072, 4, 16, 1440], P(('ens', 'trc')), may hold values from -6 to 6
- velocity: float32 [2, 4, 16, 1440], replicated, may hold values from -0.24 to 0.24
- land_mask: int32 [16, 1440], replicated, may hold values from 0 to 1, as said below
- in_weight: bfloat16 [24, 256], replicated, may hold values from -1.25 to 1.25
- bias_one: float32 [256], replicated, may hold values from -3 to 3
- hid_weight: bfloat16 [256, 256], replicated, may hold values from -0.375 to 0.375
- bias_two: float32 [256], replicated, may hold values from -3 to 3
- out_coef: float32 [128, 24, 256], P('ens'), may hold values from -6 to 6
- obs_cell: int32 [16, 128], P('trc'), may hold values from 0 to 5759, as said below
- obs_count: int32 [16], P('trc'), may hold values from 16 to 128, as said below
- obs_value: float32 [16, 6, 128], P('trc'), may hold values from -6 to 6
- obs_var: float32 [16, 6, 128], P('trc'), may hold values from 0.05 to 0.5
- obs_noise: float32 [128, 16, 6, 128], P(None, 'trc'), may hold values from -2 to 2
Outputs:
- new_state: bfloat16 [3072, 4, 16, 1440], P('ens', None, 'trc')
- new_coef: float32 [128, 24, 256], P('ens')
The draws below stay inside these ranges and needn't reach their ends.
Inputs may be any that keep to these rules, and one draw needn't show every extreme that they name: `land_mask`: every block of 1 latitude rows (rows k * 1 to (k + 1) - 1) holds at most 1152 ocean columns, and some block exactly 1152. `obs_cell`: every slot names an ocean cell of its block. `obs_count`: some block uses all 128 slots.
All inputs are finite; a program needn't handle non-finite values.
Results may differ from the reference program's by a relative error of at most 0.0068.
Values may be sent and summed in bfloat16 or wider, within the bound.
No kernel may reach another device: no remote copies, remote signals or barrier semaphores. Data moves between devices by JAX's collectives and lax.ppermute only.
A program may use at most 128 MiB of HBM per device.

```python
import math
import jax
import jax.numpy as jnp
from jax import lax

NTR = 24
HID = 256
OBS_TR = 6
LON = 1440
ROW_OCEAN = 1152
ADV_STEPS = 2
OBS_CAP = 128
LEV = 4
ROWBLK = 1
MEMBERS = 128
LATS = 16
BLOCKS = 16
COL_DEV = 1440


def land_layout(seed_key):
    key_count, key_block, key_start = jax.random.split(seed_key, 3)
    counts = jax.random.randint(key_count, (LATS,), ROW_OCEAN // 2, ROW_OCEAN + 1)
    full_block = jax.random.randint(key_block, (), 0, LATS // ROWBLK)
    row_block_ids = jnp.arange(LATS) // ROWBLK
    counts = jnp.where(row_block_ids == full_block, ROW_OCEAN, counts)
    starts = jax.random.randint(key_start, (LATS,), 0, LON)
    return (counts, starts)


def draw_land_mask(key, part):
    counts, starts = land_layout(jax.random.fold_in(key, 11))
    longitude = jnp.arange(LON)
    offset = (longitude[None, :] - starts[:, None]) % LON
    return (offset >= LON - counts[:, None]).astype(jnp.int32)


def draw_obs_cell(key, part):
    counts, starts = land_layout(jax.random.fold_in(key, 11))
    key_row, key_level, key_pos = jax.random.split(jax.random.fold_in(key, 23), 3)
    block_count = LATS // ROWBLK
    row_within = jax.random.randint(key_row, (block_count, OBS_CAP), 0, ROWBLK)
    latitude = jnp.arange(block_count)[:, None] * ROWBLK + row_within
    level_ids = jax.random.randint(key_level, (block_count, OBS_CAP), 0, LEV)
    row_counts = counts[latitude]
    ocean_pos = jax.random.randint(key_pos, (block_count, OBS_CAP), 0, row_counts)
    longitude = (starts[latitude] + LON - row_counts + ocean_pos) % LON
    return (level_ids * (ROWBLK * LON) + row_within * LON + longitude).astype(jnp.int32)


def draw_obs_count(key, part):
    key_count, key_full = jax.random.split(jax.random.fold_in(key, 37))
    block_count = LATS // ROWBLK
    counts = jax.random.randint(key_count, (block_count,), OBS_CAP // 8, OBS_CAP // 2 + 1)
    full_block = jax.random.randint(key_full, (), 0, block_count)
    return jnp.where(jnp.arange(block_count) == full_block, OBS_CAP, counts).astype(jnp.int32)


def shard_levels(stream_key, dims, cuts, least, largest):
    loudness = 1.0
    for position, blocks in cuts:
        heights = jax.random.uniform(jax.random.fold_in(jax.random.fold_in(stream_key, 6), position), (blocks,), jnp.float32, least / len(cuts), largest / len(cuts))
        loudness = loudness * jnp.repeat(jnp.exp(heights), dims[position] // blocks).reshape((-1,) + (1,) * (len(dims) - 1 - position))
    return loudness


def bell_draw(own_key, shape, scale, most, pieces=(), held_as=jnp.bfloat16):
    result = scale * jax.random.normal(own_key, shape, jnp.float32)
    if pieces:
        result = result * shard_levels(own_key, shape, pieces, -0.22, 0.18)
    return jnp.clip(result, -most, most).astype(held_as)


def setup_inputs(seed: int = 0) -> dict:
    seeds = jax.random.split(jax.random.key(seed), 14)
    tracer_state = bell_draw(seeds[0], (MEMBERS * NTR, LEV, LATS, LON), 1.0, 6.0, ((0, 128),))
    velocity = jnp.clip(jax.random.uniform(seeds[1], (2, LEV, LATS, LON), jnp.float32, -0.24, 0.24), -0.24, 0.24)
    land_mask = draw_land_mask(jax.random.fold_in(seeds[13], 71), 0)
    in_weight = bell_draw(seeds[3], (NTR, HID), NTR ** -0.5, 1.25)
    bias_one = bell_draw(seeds[4], (HID,), 0.5, 3.0, (), jnp.float32)
    hid_weight = bell_draw(seeds[5], (HID, HID), HID ** -0.5, 0.375)
    bias_two = bell_draw(seeds[6], (HID,), 0.5, 3.0, (), jnp.float32)
    out_coef = bell_draw(seeds[7], (MEMBERS, NTR, HID), 1.0, 6.0, ((0, 8),), jnp.float32)
    obs_cell = draw_obs_cell(jax.random.fold_in(seeds[13], 71), 0)
    obs_count = draw_obs_count(jax.random.fold_in(seeds[13], 71), 0)
    obs_value = bell_draw(seeds[10], (BLOCKS, OBS_TR, OBS_CAP), 1.0, 6.0, ((0, 16),), jnp.float32)
    obs_var = jnp.clip(jnp.exp(math.log(0.5) - 2.3025851 * jax.random.uniform(seeds[11], (BLOCKS, OBS_TR, OBS_CAP), jnp.float32) ** shard_levels(seeds[11], (BLOCKS, OBS_TR, OBS_CAP), ((0, 16),), -0.2, 0.2)), 0.05, 0.5)
    obs_noise = bell_draw(seeds[12], (MEMBERS, BLOCKS, OBS_TR, OBS_CAP), 0.3, 2.0, ((1, 16),), jnp.float32)
    return dict(tracer_state=tracer_state, velocity=velocity, land_mask=land_mask, in_weight=in_weight, bias_one=bias_one, hid_weight=hid_weight, bias_two=bias_two, out_coef=out_coef, obs_cell=obs_cell, obs_count=obs_count, obs_value=obs_value, obs_var=obs_var, obs_noise=obs_noise)


def transport(concentration, velocity, sea_mask):
    east_open = sea_mask * jnp.roll(sea_mask, -1, axis=1)
    north_open = sea_mask * jnp.concatenate([sea_mask[1:], jnp.zeros_like(sea_mask[:1])], axis=0)
    east_speed = velocity[0] * east_open
    north_speed = velocity[1] * north_open
    for _ in range(ADV_STEPS):
        east_value = jnp.roll(concentration, -1, axis=-1)
        east_flux = jnp.maximum(east_speed, 0.0) * concentration + jnp.minimum(east_speed, 0.0) * east_value
        north_value = jnp.concatenate([concentration[..., 1:, :], jnp.zeros_like(concentration[..., :1, :])], axis=-2)
        north_flux = jnp.maximum(north_speed, 0.0) * concentration + jnp.minimum(north_speed, 0.0) * north_value
        west_flux = jnp.roll(east_flux, 1, axis=-1)
        south_flux = jnp.concatenate([jnp.zeros_like(north_flux[..., :1, :]), north_flux[..., :-1, :]], axis=-2)
        concentration = concentration - (east_flux - west_flux) - (north_flux - south_flux)
    return concentration

def reaction(fields, in_weight, bias_one, hid_weight, bias_two, member_coef, sea_cells):
    contract = (((0,), (0,)), ((), ()))
    hidden_one = lax.dot_general(in_weight.astype(jnp.float32), fields.astype(jnp.float32), contract, preferred_element_type=jnp.float32)
    hidden_one = jax.nn.silu(hidden_one + bias_one[:, None]).astype(jnp.bfloat16)
    hidden_two = lax.dot_general(hid_weight.astype(jnp.float32), hidden_one.astype(jnp.float32), contract, preferred_element_type=jnp.float32)
    hidden_two = jax.nn.silu(hidden_two + bias_two[:, None]).astype(jnp.bfloat16)
    tendency = jnp.dot(member_coef.astype(jnp.float32), hidden_two.astype(jnp.float32), preferred_element_type=jnp.float32) * hid_weight.shape[0] ** (-0.5)
    return ((fields.astype(jnp.float32) + tendency) * sea_cells).astype(jnp.bfloat16)

def solve_system(system, right_side):
    factor = jnp.linalg.cholesky(system)
    middle = lax.linalg.triangular_solve(factor, right_side, left_side=True, lower=True)
    return lax.linalg.triangular_solve(factor, middle, left_side=True, lower=True, transpose_a=True)

def reference(tracer_state, velocity, land_mask, in_weight, bias_one, hid_weight, bias_two, out_coef, obs_cell, obs_count, obs_value, obs_var, obs_noise):
    sea_mask = land_mask.astype(jnp.float32)
    fields_all = tracer_state.reshape(MEMBERS, NTR, LEV, LATS, LON)
    coef_half = out_coef.astype(jnp.bfloat16)
    sea_cells = jnp.broadcast_to(sea_mask[None], (LEV, LATS, LON)).reshape(-1)
    cell_index = jnp.broadcast_to(obs_cell[:, None, :], (BLOCKS, OBS_TR, OBS_CAP))

    def one_member(inputs):
        member_state, member_coef = inputs
        advected = transport(member_state.astype(jnp.float32) * sea_mask, velocity, sea_mask).astype(jnp.bfloat16)
        reacted = reaction(advected.reshape(NTR, -1), in_weight, bias_one, hid_weight, bias_two, member_coef, sea_cells)
        reacted = reacted.reshape(NTR, LEV, LATS, LON)
        observed = reacted[:OBS_TR].reshape(OBS_TR, LEV, BLOCKS, COL_DEV)
        observed = jnp.transpose(observed, (2, 0, 1, 3)).reshape(BLOCKS, OBS_TR, LEV * COL_DEV)
        picked = jnp.take_along_axis(observed, cell_index, axis=2)
        return (reacted, picked)
    new_fields, predicted = lax.map(one_member, (fields_all, coef_half))
    slot_ids = jnp.arange(OBS_CAP, dtype=jnp.int32)
    valid_slots = (slot_ids[None, :] < obs_count[:, None]).astype(jnp.float32)
    weight = valid_slots[:, None, :] / obs_var
    guessed = predicted.astype(jnp.float32).reshape(MEMBERS, -1)
    anomaly = guessed - jnp.mean(guessed, axis=0)
    misfit = (obs_value[None] + obs_noise).reshape(MEMBERS, -1) - guessed
    weighted = anomaly * weight.reshape(1, -1)
    highest = lax.Precision.HIGHEST
    gram = jnp.dot(weighted.astype(jnp.float32), anomaly.T.astype(jnp.float32), precision=highest, preferred_element_type=jnp.float32)
    cross = jnp.dot(weighted.astype(jnp.float32), misfit.T.astype(jnp.float32), precision=highest, preferred_element_type=jnp.float32)
    system = (MEMBERS - 1) * jnp.eye(MEMBERS, dtype=jnp.float32) + gram
    mixing = solve_system(system, cross)
    flat_coef = out_coef.reshape(MEMBERS, -1)
    new_coef = flat_coef + jnp.dot(mixing.T.astype(jnp.float32), flat_coef.astype(jnp.float32), precision=highest, preferred_element_type=jnp.float32)
    new_state = new_fields.reshape(MEMBERS * NTR, LEV, LATS, LON)
    return (new_state, new_coef.reshape(MEMBERS, NTR, HID))
```

```python
import jax
import jax.numpy as jnp
from jax import lax
from jax.sharding import PartitionSpec as P

OBS_TR = 6
ADV_STEPS = 2
OBS_CAP = 128


def transport(concentration, velocity, sea_mask):
    east_open = sea_mask * jnp.roll(sea_mask, -1, axis=1)
    north_open = sea_mask * jnp.concatenate([sea_mask[1:], jnp.zeros_like(sea_mask[:1])], axis=0)
    east_speed = velocity[0] * east_open
    north_speed = velocity[1] * north_open
    for _ in range(ADV_STEPS):
        east_value = jnp.roll(concentration, -1, axis=-1)
        east_flux = (
            jnp.maximum(east_speed, 0.0) * concentration + jnp.minimum(east_speed, 0.0) * east_value
        )
        north_value = jnp.concatenate(
            [concentration[..., 1:, :], jnp.zeros_like(concentration[..., :1, :])], axis=-2
        )
        north_flux = (
            jnp.maximum(north_speed, 0.0) * concentration
            + jnp.minimum(north_speed, 0.0) * north_value
        )
        west_flux = jnp.roll(east_flux, 1, axis=-1)
        south_flux = jnp.concatenate(
            [jnp.zeros_like(north_flux[..., :1, :]), north_flux[..., :-1, :]], axis=-2
        )
        concentration = concentration - (east_flux - west_flux) - (north_flux - south_flux)
    return concentration


def silu(value):
    return value * (0.5 + 0.5 * jnp.tanh(0.5 * value))


def tree_sum(value, axis_name, size):
    if size & (size - 1):
        return lax.psum(value, axis_name)
    step = 1
    while step < size:
        pairs = [(i, i ^ step) for i in range(size)]
        value = value + lax.ppermute(value, axis_name, pairs)
        step *= 2
    return value


def reaction(fields, in_weight, bias_one, hid_weight, bias_two, member_coef, sea_cells):
    contract = (((0,), (0,)), ((), ()))
    hidden_one = lax.dot_general(in_weight, fields, contract, preferred_element_type=jnp.float32)
    hidden_one = silu(hidden_one + bias_one[:, None]).astype(jnp.bfloat16)
    hidden_two = lax.dot_general(
        hid_weight, hidden_one, contract, preferred_element_type=jnp.float32
    )
    hidden_two = silu(hidden_two + bias_two[:, None]).astype(jnp.bfloat16)
    tendency = jnp.dot(
        member_coef, hidden_two, preferred_element_type=jnp.float32
    ) * hid_weight.shape[0] ** (-0.5)
    return ((fields.astype(jnp.float32) + tendency) * sea_cells).astype(jnp.bfloat16)


def solve_system(system, right_side):
    factor = jnp.linalg.cholesky(system)
    middle = lax.linalg.triangular_solve(factor, right_side, left_side=True, lower=True)
    return lax.linalg.triangular_solve(factor, middle, left_side=True, lower=True, transpose_a=True)


def shards(
    tracer_state,
    velocity,
    land_mask,
    in_weight,
    bias_one,
    hid_weight,
    bias_two,
    out_coef,
    obs_cell,
    obs_count,
    obs_value,
    obs_var,
    obs_noise,
):
    blocks = lax.axis_size("trc")
    own_block = lax.axis_index("trc")
    group_index = lax.axis_index("ens")
    field_rows, levels, lat_rows, lon_count = tracer_state.shape
    row_block = lat_rows // blocks
    block_width = row_block * lon_count
    members_here = out_coef.shape[0]
    tracers = in_weight.shape[0]
    group_rows = members_here * tracers
    highest = lax.Precision.HIGHEST
    sea_mask = land_mask.astype(jnp.float32)
    coef_all = lax.all_gather(out_coef.reshape(out_coef.shape[0], -1), "ens", axis=0, tiled=True)
    advected = transport(tracer_state.astype(jnp.float32) * sea_mask, velocity, sea_mask).astype(
        jnp.bfloat16
    )
    coef_half = out_coef.astype(jnp.bfloat16)
    sea_own = lax.dynamic_slice_in_dim(sea_mask, own_block * row_block, row_block, 0)
    gathered = lax.all_to_all(advected, "trc", split_axis=2, concat_axis=0, tiled=True)
    out_shape = gathered.shape
    grouped = gathered.reshape(members_here, tracers, -1)
    sea_cells = jnp.broadcast_to(sea_own[None], (out_shape[1],) + sea_own.shape).reshape(-1)

    def one_member(inputs):
        fields, member_coef = inputs
        return reaction(fields, in_weight, bias_one, hid_weight, bias_two, member_coef, sea_cells)

    reacted = lax.map(one_member, (grouped, coef_half))
    new_cols = reacted.reshape(out_shape)
    new_flat = new_cols.reshape(group_rows, levels, block_width)
    observed = new_flat.reshape(members_here, tracers, levels * block_width)[:, :OBS_TR]
    observed = observed.reshape(members_here * OBS_TR, levels * block_width)
    cell_ids = lax.broadcasted_iota(jnp.int32, (levels * block_width, OBS_CAP), 0)
    picker = (cell_ids == obs_cell[0][None, :]).astype(jnp.bfloat16)
    picked = jnp.dot(observed, picker, preferred_element_type=jnp.float32)
    predicted_own = picked.astype(jnp.bfloat16).reshape(members_here, OBS_TR, OBS_CAP)
    predicted_all = lax.all_gather(predicted_own, "ens", axis=0, tiled=True)
    member_total = predicted_all.shape[0]
    slot_ids = jnp.arange(OBS_CAP, dtype=jnp.int32)
    valid_slots = (slot_ids < obs_count[0]).astype(jnp.float32)
    weight = valid_slots[None, :] / obs_var[0]
    guessed = predicted_all.astype(jnp.float32).reshape(member_total, -1)
    anomaly = guessed - jnp.mean(guessed, axis=0)
    misfit = (obs_value[None] + obs_noise).reshape(member_total, -1) - guessed
    weighted = anomaly * weight.reshape(1, -1)
    gram_part = jnp.dot(weighted, anomaly.T, precision=highest, preferred_element_type=jnp.float32)
    cross_part = jnp.dot(weighted, misfit.T, precision=highest, preferred_element_type=jnp.float32)
    both = tree_sum(jnp.stack([gram_part, cross_part]), "trc", blocks)
    gram, cross = both[0], both[1]
    system = (member_total - 1) * jnp.eye(member_total, dtype=jnp.float32) + gram
    mixing = solve_system(system, cross)
    flat_coef = out_coef.reshape(members_here, -1)
    first_member = group_index * members_here
    mixing_cols = lax.dynamic_slice_in_dim(mixing, first_member, members_here, 1)
    summed = jnp.dot(mixing_cols.T, coef_all, precision=highest, preferred_element_type=jnp.float32)
    new_coef = flat_coef + summed
    return (new_cols, new_coef.reshape(members_here, tracers, -1))


def solution(mesh):
    in_specs = (
        P(("ens", "trc"), None, None, None),
        P(),
        P(),
        P(),
        P(),
        P(),
        P(),
        P("ens", None, None),
        P("trc", None),
        P("trc"),
        P("trc", None, None),
        P("trc", None, None),
        P(None, "trc", None, None),
    )
    out_specs = (P("ens", None, "trc", None), P("ens", None, None))
    return jax.shard_map(shards, mesh=mesh, in_specs=in_specs, out_specs=out_specs, check_vma=False)
```

```python
import jax
import jax.numpy as jnp
from jax import lax
from jax.sharding import PartitionSpec as P

OBS_TR = 6
ADV_STEPS = 2
OBS_CAP = 128


def transport(concentration, velocity, sea_mask):
    east_open = sea_mask * jnp.roll(sea_mask, -1, axis=1)
    north_open = sea_mask * jnp.concatenate([sea_mask[1:], jnp.zeros_like(sea_mask[:1])], axis=0)
    east_speed = velocity[0] * east_open
    north_speed = velocity[1] * north_open
    for _ in range(ADV_STEPS):
        east_value = jnp.roll(concentration, -1, axis=-1)
        east_flux = (
            jnp.maximum(east_speed, 0.0) * concentration + jnp.minimum(east_speed, 0.0) * east_value
        )
        north_value = jnp.concatenate(
            [concentration[..., 1:, :], jnp.zeros_like(concentration[..., :1, :])], axis=-2
        )
        north_flux = (
            jnp.maximum(north_speed, 0.0) * concentration
            + jnp.minimum(north_speed, 0.0) * north_value
        )
        west_flux = jnp.roll(east_flux, 1, axis=-1)
        south_flux = jnp.concatenate(
            [jnp.zeros_like(north_flux[..., :1, :]), north_flux[..., :-1, :]], axis=-2
        )
        concentration = concentration - (east_flux - west_flux) - (north_flux - south_flux)
    return concentration


def silu(value):
    return value * (0.5 + 0.5 * jnp.tanh(0.5 * value))


def tree_sum(value, axis_name, size):
    if size & (size - 1):
        return lax.psum(value, axis_name)
    step = 1
    while step < size:
        pairs = [(i, i ^ step) for i in range(size)]
        value = value + lax.ppermute(value, axis_name, pairs)
        step *= 2
    return value


def reaction(fields, in_weight, bias_one, hid_weight, bias_two, member_coef, sea_cells):
    contract = (((0,), (0,)), ((), ()))
    hidden_one = lax.dot_general(in_weight, fields, contract, preferred_element_type=jnp.float32)
    hidden_one = silu(hidden_one + bias_one[:, None]).astype(jnp.bfloat16)
    hidden_two = lax.dot_general(
        hid_weight, hidden_one, contract, preferred_element_type=jnp.float32
    )
    hidden_two = silu(hidden_two + bias_two[:, None]).astype(jnp.bfloat16)
    tendency = jnp.dot(
        member_coef, hidden_two, preferred_element_type=jnp.float32
    ) * hid_weight.shape[0] ** (-0.5)
    return ((fields.astype(jnp.float32) + tendency) * sea_cells).astype(jnp.bfloat16)


def solve_system(system, right_side):
    factor = jnp.linalg.cholesky(system)
    middle = lax.linalg.triangular_solve(factor, right_side, left_side=True, lower=True)
    return lax.linalg.triangular_solve(factor, middle, left_side=True, lower=True, transpose_a=True)


def shards(
    tracer_state,
    velocity,
    land_mask,
    in_weight,
    bias_one,
    hid_weight,
    bias_two,
    out_coef,
    obs_cell,
    obs_count,
    obs_value,
    obs_var,
    obs_noise,
):
    blocks = lax.axis_size("trc")
    own_block = lax.axis_index("trc")
    group_index = lax.axis_index("ens")
    field_rows, levels, lat_rows, lon_count = tracer_state.shape
    row_block = lat_rows // blocks
    block_width = row_block * lon_count
    members_here = out_coef.shape[0]
    tracers = in_weight.shape[0]
    group_rows = members_here * tracers
    highest = lax.Precision.HIGHEST
    sea_mask = land_mask.astype(jnp.float32)
    coef_all = lax.all_gather(out_coef.reshape(out_coef.shape[0], -1), "ens", axis=0, tiled=True)
    coef_half = out_coef.astype(jnp.bfloat16)
    sea_own = lax.dynamic_slice_in_dim(sea_mask, own_block * row_block, row_block, 0)
    sea_flat = sea_own.reshape(-1)
    scale = hid_weight.shape[0] ** (-0.5)
    level_cells = lax.broadcasted_iota(jnp.int32, (block_width, OBS_CAP), 0)
    picked = jnp.zeros((members_here * OBS_TR, OBS_CAP), jnp.float32)
    level_outs = []
    for level in range(levels):
        state = tracer_state[:, level].astype(jnp.float32) * sea_mask
        advected = transport(state, velocity[:, level], sea_mask).astype(jnp.bfloat16)
        gathered = lax.all_to_all(advected, "trc", split_axis=1, concat_axis=0, tiled=True)
        fields = gathered.reshape(members_here, tracers, block_width)
        hidden_one = jnp.einsum(
            "tk,mtc->mkc", in_weight, fields, preferred_element_type=jnp.float32
        )
        hidden_one = silu(hidden_one + bias_one[None, :, None]).astype(jnp.bfloat16)
        hidden_two = jnp.einsum(
            "jk,mjc->mkc", hid_weight, hidden_one, preferred_element_type=jnp.float32
        )
        hidden_two = silu(hidden_two + bias_two[None, :, None]).astype(jnp.bfloat16)
        tendency = jnp.einsum(
            "mtk,mkc->mtc", coef_half, hidden_two, preferred_element_type=jnp.float32
        ) * scale
        reacted = ((fields.astype(jnp.float32) + tendency) * sea_flat).astype(jnp.bfloat16)
        level_outs.append(reacted.reshape(group_rows, row_block, lon_count))
        observed = reacted[:, :OBS_TR].reshape(members_here * OBS_TR, block_width)
        picker = (level_cells + level * block_width == obs_cell[0][None, :]).astype(jnp.bfloat16)
        picked = picked + jnp.dot(observed, picker, preferred_element_type=jnp.float32)
    new_cols = jnp.stack(level_outs, axis=1)
    predicted_own = picked.astype(jnp.bfloat16).reshape(members_here, OBS_TR, OBS_CAP)
    predicted_all = lax.all_gather(predicted_own, "ens", axis=0, tiled=True)
    member_total = predicted_all.shape[0]
    slot_ids = jnp.arange(OBS_CAP, dtype=jnp.int32)
    valid_slots = (slot_ids < obs_count[0]).astype(jnp.float32)
    weight = valid_slots[None, :] / obs_var[0]
    guessed = predicted_all.astype(jnp.float32).reshape(member_total, -1)
    anomaly = guessed - jnp.mean(guessed, axis=0)
    misfit = (obs_value[None] + obs_noise).reshape(member_total, -1) - guessed
    weighted = anomaly * weight.reshape(1, -1)
    gram_part = jnp.dot(weighted, anomaly.T, precision=highest, preferred_element_type=jnp.float32)
    cross_part = jnp.dot(weighted, misfit.T, precision=highest, preferred_element_type=jnp.float32)
    both = tree_sum(jnp.stack([gram_part, cross_part]), "trc", blocks)
    gram, cross = both[0], both[1]
    system = (member_total - 1) * jnp.eye(member_total, dtype=jnp.float32) + gram
    mixing = solve_system(system, cross)
    flat_coef = out_coef.reshape(members_here, -1)
    first_member = group_index * members_here
    mixing_cols = lax.dynamic_slice_in_dim(mixing, first_member, members_here, 1)
    summed = jnp.dot(mixing_cols.T, coef_all, precision=highest, preferred_element_type=jnp.float32)
    new_coef = flat_coef + summed
    return (new_cols, new_coef.reshape(members_here, tracers, -1))


def solution(mesh):
    in_specs = (
        P(("ens", "trc"), None, None, None),
        P(),
        P(),
        P(),
        P(),
        P(),
        P(),
        P("ens", None, None),
        P("trc", None),
        P("trc"),
        P("trc", None, None),
        P("trc", None, None),
        P(None, "trc", None, None),
    )
    out_specs = (P("ens", None, "trc", None), P("ens", None, None))
    return jax.shard_map(shards, mesh=mesh, in_specs=in_specs, out_specs=out_specs, check_vma=False)
```

```python
import jax
import jax.numpy as jnp
from jax import lax
from jax.sharding import PartitionSpec as P

OBS_TR = 6
ADV_STEPS = 2
OBS_CAP = 128


def transport(concentration, velocity, sea_mask):
    east_open = sea_mask * jnp.roll(sea_mask, -1, axis=1)
    north_open = sea_mask * jnp.concatenate([sea_mask[1:], jnp.zeros_like(sea_mask[:1])], axis=0)
    east_speed = velocity[0] * east_open
    north_speed = velocity[1] * north_open
    for _ in range(ADV_STEPS):
        east_value = jnp.roll(concentration, -1, axis=-1)
        east_flux = (
            jnp.maximum(east_speed, 0.0) * concentration + jnp.minimum(east_speed, 0.0) * east_value
        )
        north_value = jnp.concatenate(
            [concentration[..., 1:, :], jnp.zeros_like(concentration[..., :1, :])], axis=-2
        )
        north_flux = (
            jnp.maximum(north_speed, 0.0) * concentration
            + jnp.minimum(north_speed, 0.0) * north_value
        )
        west_flux = jnp.roll(east_flux, 1, axis=-1)
        south_flux = jnp.concatenate(
            [jnp.zeros_like(north_flux[..., :1, :]), north_flux[..., :-1, :]], axis=-2
        )
        concentration = concentration - (east_flux - west_flux) - (north_flux - south_flux)
    return concentration


def silu(value):
    return value * (0.5 + 0.5 * jnp.tanh(0.5 * value))


def tree_sum(value, axis_name, size):
    if size & (size - 1):
        return lax.psum(value, axis_name)
    step = 1
    while step < size:
        pairs = [(i, i ^ step) for i in range(size)]
        value = value + lax.ppermute(value, axis_name, pairs)
        step *= 2
    return value


def reaction(fields, in_weight, bias_one, hid_weight, bias_two, member_coef, sea_cells):
    contract = (((0,), (0,)), ((), ()))
    hidden_one = lax.dot_general(in_weight, fields, contract, preferred_element_type=jnp.float32)
    hidden_one = silu(hidden_one + bias_one[:, None]).astype(jnp.bfloat16)
    hidden_two = lax.dot_general(
        hid_weight, hidden_one, contract, preferred_element_type=jnp.float32
    )
    hidden_two = silu(hidden_two + bias_two[:, None]).astype(jnp.bfloat16)
    tendency = jnp.dot(
        member_coef, hidden_two, preferred_element_type=jnp.float32
    ) * hid_weight.shape[0] ** (-0.5)
    return ((fields.astype(jnp.float32) + tendency) * sea_cells).astype(jnp.bfloat16)


def react_batch(fields, in_weight, bias_one, hid_weight, bias_two, coef_half, sea_cells):
    hidden_one = jnp.einsum("tk,mtc->mkc", in_weight, fields, preferred_element_type=jnp.float32)
    hidden_one = silu(hidden_one + bias_one[None, :, None]).astype(jnp.bfloat16)
    hidden_two = jnp.einsum(
        "jk,mjc->mkc", hid_weight, hidden_one, preferred_element_type=jnp.float32
    )
    hidden_two = silu(hidden_two + bias_two[None, :, None]).astype(jnp.bfloat16)
    tendency = jnp.einsum(
        "mtk,mkc->mtc", coef_half, hidden_two, preferred_element_type=jnp.float32
    ) * hid_weight.shape[0] ** (-0.5)
    return ((fields.astype(jnp.float32) + tendency) * sea_cells).astype(jnp.bfloat16)


def solve_system(system, right_side):
    factor = jnp.linalg.cholesky(system)
    middle = lax.linalg.triangular_solve(factor, right_side, left_side=True, lower=True)
    return lax.linalg.triangular_solve(factor, middle, left_side=True, lower=True, transpose_a=True)


def shards(
    tracer_state,
    velocity,
    land_mask,
    in_weight,
    bias_one,
    hid_weight,
    bias_two,
    out_coef,
    obs_cell,
    obs_count,
    obs_value,
    obs_var,
    obs_noise,
):
    blocks = lax.axis_size("trc")
    own_block = lax.axis_index("trc")
    group_index = lax.axis_index("ens")
    field_rows, levels, lat_rows, lon_count = tracer_state.shape
    row_block = lat_rows // blocks
    block_width = row_block * lon_count
    members_here = out_coef.shape[0]
    tracers = in_weight.shape[0]
    group_rows = members_here * tracers
    highest = lax.Precision.HIGHEST
    sea_mask = land_mask.astype(jnp.float32)
    coef_all = lax.all_gather(out_coef.reshape(out_coef.shape[0], -1), "ens", axis=0, tiled=True)
    coef_half = out_coef.astype(jnp.bfloat16)
    sea_own = lax.dynamic_slice_in_dim(sea_mask, own_block * row_block, row_block, 0)
    sea_flat = sea_own.reshape(-1)
    scale = hid_weight.shape[0] ** (-0.5)
    level_cells = lax.broadcasted_iota(jnp.int32, (block_width, OBS_CAP), 0)
    within = (level_cells == (obs_cell[0] % block_width)[None, :]).astype(jnp.bfloat16)
    sea_obs = jnp.dot(sea_flat.astype(jnp.bfloat16), within, preferred_element_type=jnp.float32)
    obs_fields = jnp.zeros((members_here, tracers, OBS_CAP), jnp.float32)
    level_outs = []
    for level in range(levels):
        state = tracer_state[:, level].astype(jnp.float32) * sea_mask
        advected = transport(state, velocity[:, level], sea_mask).astype(jnp.bfloat16)
        gathered = lax.all_to_all(advected, "trc", split_axis=1, concat_axis=0, tiled=True)
        fields = gathered.reshape(members_here, tracers, block_width)
        picker = (level_cells + level * block_width == obs_cell[0][None, :]).astype(jnp.bfloat16)
        obs_fields = obs_fields + jnp.einsum(
            "mtc,cs->mts", fields, picker, preferred_element_type=jnp.float32
        )
        reacted = react_batch(fields, in_weight, bias_one, hid_weight, bias_two, coef_half, sea_flat)
        level_outs.append(reacted.reshape(group_rows, row_block, lon_count))
    new_cols = jnp.stack(level_outs, axis=1)
    obs_x = obs_fields.astype(jnp.bfloat16)
    obs_new = react_batch(obs_x, in_weight, bias_one, hid_weight, bias_two, coef_half, sea_obs)
    predicted_own = obs_new[:, :OBS_TR]
    predicted_all = lax.all_gather(predicted_own, "ens", axis=0, tiled=True)
    member_total = predicted_all.shape[0]
    slot_ids = jnp.arange(OBS_CAP, dtype=jnp.int32)
    valid_slots = (slot_ids < obs_count[0]).astype(jnp.float32)
    weight = valid_slots[None, :] / obs_var[0]
    guessed = predicted_all.astype(jnp.float32).reshape(member_total, -1)
    anomaly = guessed - jnp.mean(guessed, axis=0)
    misfit = (obs_value[None] + obs_noise).reshape(member_total, -1) - guessed
    weighted = anomaly * weight.reshape(1, -1)
    gram_part = jnp.dot(weighted, anomaly.T, precision=highest, preferred_element_type=jnp.float32)
    cross_part = jnp.dot(weighted, misfit.T, precision=highest, preferred_element_type=jnp.float32)
    both = tree_sum(jnp.stack([gram_part, cross_part]), "trc", blocks)
    gram, cross = both[0], both[1]
    system = (member_total - 1) * jnp.eye(member_total, dtype=jnp.float32) + gram
    mixing = solve_system(system, cross)
    flat_coef = out_coef.reshape(members_here, -1)
    first_member = group_index * members_here
    mixing_cols = lax.dynamic_slice_in_dim(mixing, first_member, members_here, 1)
    summed = jnp.dot(mixing_cols.T, coef_all, precision=highest, preferred_element_type=jnp.float32)
    new_coef = flat_coef + summed
    return (new_cols, new_coef.reshape(members_here, tracers, -1))


def solution(mesh):
    in_specs = (
        P(("ens", "trc"), None, None, None),
        P(),
        P(),
        P(),
        P(),
        P(),
        P(),
        P("ens", None, None),
        P("trc", None),
        P("trc"),
        P("trc", None, None),
        P("trc", None, None),
        P(None, "trc", None, None),
    )
    out_specs = (P("ens", None, "trc", None), P("ens", None, None))
    return jax.shard_map(shards, mesh=mesh, in_specs=in_specs, out_specs=out_specs, check_vma=False)
```

```python
import jax
import jax.numpy as jnp
from jax import lax
from jax.sharding import PartitionSpec as P

OBS_TR = 6
ADV_STEPS = 2
OBS_CAP = 128


def transport(concentration, velocity, sea_mask):
    east_open = sea_mask * jnp.roll(sea_mask, -1, axis=1)
    north_open = sea_mask * jnp.concatenate([sea_mask[1:], jnp.zeros_like(sea_mask[:1])], axis=0)
    east_speed = velocity[0] * east_open
    north_speed = velocity[1] * north_open
    for _ in range(ADV_STEPS):
        east_value = jnp.roll(concentration, -1, axis=-1)
        east_flux = (
            jnp.maximum(east_speed, 0.0) * concentration + jnp.minimum(east_speed, 0.0) * east_value
        )
        north_value = jnp.concatenate(
            [concentration[..., 1:, :], jnp.zeros_like(concentration[..., :1, :])], axis=-2
        )
        north_flux = (
            jnp.maximum(north_speed, 0.0) * concentration
            + jnp.minimum(north_speed, 0.0) * north_value
        )
        west_flux = jnp.roll(east_flux, 1, axis=-1)
        south_flux = jnp.concatenate(
            [jnp.zeros_like(north_flux[..., :1, :]), north_flux[..., :-1, :]], axis=-2
        )
        concentration = concentration - (east_flux - west_flux) - (north_flux - south_flux)
    return concentration


def shift_lat(field, offset):
    zeros = jnp.zeros_like(field[..., :1, :])
    if offset > 0:
        return jnp.concatenate([field[..., 1:, :], zeros], axis=-2)
    return jnp.concatenate([zeros, field[..., :-1, :]], axis=-2)


def transport_stencil(concentration, velocity, sea_mask):
    east_open = sea_mask * jnp.roll(sea_mask, -1, axis=1)
    north_open = sea_mask * shift_lat(sea_mask, 1)
    east_speed = velocity[0] * east_open
    north_speed = velocity[1] * north_open
    east_out = jnp.maximum(east_speed, 0.0)
    east_in = jnp.minimum(east_speed, 0.0)
    north_out = jnp.maximum(north_speed, 0.0)
    north_in = jnp.minimum(north_speed, 0.0)
    west_out = jnp.roll(east_out, 1, axis=-1)
    west_in = jnp.roll(east_in, 1, axis=-1)
    south_out = shift_lat(north_out, -1)
    south_in = shift_lat(north_in, -1)
    centre = 1.0 - east_out + west_in - north_out + south_in
    for _ in range(ADV_STEPS):
        concentration = (
            centre * concentration
            - east_in * jnp.roll(concentration, -1, axis=-1)
            + west_out * jnp.roll(concentration, 1, axis=-1)
            - north_in * shift_lat(concentration, 1)
            + south_out * shift_lat(concentration, -1)
        )
    return concentration


def silu(value):
    return value * (0.5 + 0.5 * jnp.tanh(0.5 * value))


def tree_sum(value, axis_name, size):
    if size & (size - 1):
        return lax.psum(value, axis_name)
    step = 1
    while step < size:
        pairs = [(i, i ^ step) for i in range(size)]
        value = value + lax.ppermute(value, axis_name, pairs)
        step *= 2
    return value


def reaction(fields, in_weight, bias_one, hid_weight, bias_two, member_coef, sea_cells):
    contract = (((0,), (0,)), ((), ()))
    hidden_one = lax.dot_general(in_weight, fields, contract, preferred_element_type=jnp.float32)
    hidden_one = silu(hidden_one + bias_one[:, None]).astype(jnp.bfloat16)
    hidden_two = lax.dot_general(
        hid_weight, hidden_one, contract, preferred_element_type=jnp.float32
    )
    hidden_two = silu(hidden_two + bias_two[:, None]).astype(jnp.bfloat16)
    tendency = jnp.dot(
        member_coef, hidden_two, preferred_element_type=jnp.float32
    ) * hid_weight.shape[0] ** (-0.5)
    return ((fields.astype(jnp.float32) + tendency) * sea_cells).astype(jnp.bfloat16)


def solve_system(system, right_side):
    factor = jnp.linalg.cholesky(system)
    middle = lax.linalg.triangular_solve(factor, right_side, left_side=True, lower=True)
    return lax.linalg.triangular_solve(factor, middle, left_side=True, lower=True, transpose_a=True)


def shards(
    tracer_state,
    velocity,
    land_mask,
    in_weight,
    bias_one,
    hid_weight,
    bias_two,
    out_coef,
    obs_cell,
    obs_count,
    obs_value,
    obs_var,
    obs_noise,
):
    blocks = lax.axis_size("trc")
    own_block = lax.axis_index("trc")
    group_index = lax.axis_index("ens")
    field_rows, levels, lat_rows, lon_count = tracer_state.shape
    row_block = lat_rows // blocks
    block_width = row_block * lon_count
    members_here = out_coef.shape[0]
    tracers = in_weight.shape[0]
    group_rows = members_here * tracers
    highest = lax.Precision.HIGHEST
    sea_mask = land_mask.astype(jnp.float32)
    coef_all = lax.all_gather(out_coef.reshape(out_coef.shape[0], -1), "ens", axis=0, tiled=True)
    coef_half = out_coef.astype(jnp.bfloat16)
    sea_own = lax.dynamic_slice_in_dim(sea_mask, own_block * row_block, row_block, 0)
    sea_flat = sea_own.reshape(-1)
    scale = hid_weight.shape[0] ** (-0.5)
    level_cells = lax.broadcasted_iota(jnp.int32, (block_width, OBS_CAP), 0)
    picked = jnp.zeros((members_here * OBS_TR, OBS_CAP), jnp.float32)
    level_outs = []
    for level in range(levels):
        state = tracer_state[:, level].astype(jnp.float32) * sea_mask
        advected = transport_stencil(state, velocity[:, level], sea_mask).astype(jnp.bfloat16)
        gathered = lax.all_to_all(advected, "trc", split_axis=1, concat_axis=0, tiled=True)
        fields = gathered.reshape(members_here, tracers, block_width)
        hidden_one = jnp.einsum(
            "tk,mtc->mkc", in_weight, fields, preferred_element_type=jnp.float32
        )
        hidden_one = silu(hidden_one + bias_one[None, :, None]).astype(jnp.bfloat16)
        hidden_two = jnp.einsum(
            "jk,mjc->mkc", hid_weight, hidden_one, preferred_element_type=jnp.float32
        )
        hidden_two = silu(hidden_two + bias_two[None, :, None]).astype(jnp.bfloat16)
        tendency = jnp.einsum(
            "mtk,mkc->mtc", coef_half, hidden_two, preferred_element_type=jnp.float32
        ) * scale
        reacted = ((fields.astype(jnp.float32) + tendency) * sea_flat).astype(jnp.bfloat16)
        level_outs.append(reacted.reshape(group_rows, row_block, lon_count))
        observed = reacted[:, :OBS_TR].reshape(members_here * OBS_TR, block_width)
        picker = (level_cells + level * block_width == obs_cell[0][None, :]).astype(jnp.bfloat16)
        picked = picked + jnp.dot(observed, picker, preferred_element_type=jnp.float32)
    new_cols = jnp.stack(level_outs, axis=1)
    predicted_own = picked.astype(jnp.bfloat16).reshape(members_here, OBS_TR, OBS_CAP)
    predicted_all = lax.all_gather(predicted_own, "ens", axis=0, tiled=True)
    member_total = predicted_all.shape[0]
    slot_ids = jnp.arange(OBS_CAP, dtype=jnp.int32)
    valid_slots = (slot_ids < obs_count[0]).astype(jnp.float32)
    weight = valid_slots[None, :] / obs_var[0]
    guessed = predicted_all.astype(jnp.float32).reshape(member_total, -1)
    anomaly = guessed - jnp.mean(guessed, axis=0)
    misfit = (obs_value[None] + obs_noise).reshape(member_total, -1) - guessed
    weighted = anomaly * weight.reshape(1, -1)
    gram_part = jnp.dot(weighted, anomaly.T, precision=highest, preferred_element_type=jnp.float32)
    cross_part = jnp.dot(weighted, misfit.T, precision=highest, preferred_element_type=jnp.float32)
    both = tree_sum(jnp.stack([gram_part, cross_part]), "trc", blocks)
    gram, cross = both[0], both[1]
    system = (member_total - 1) * jnp.eye(member_total, dtype=jnp.float32) + gram
    mixing = solve_system(system, cross)
    flat_coef = out_coef.reshape(members_here, -1)
    first_member = group_index * members_here
    mixing_cols = lax.dynamic_slice_in_dim(mixing, first_member, members_here, 1)
    summed = jnp.dot(mixing_cols.T, coef_all, precision=highest, preferred_element_type=jnp.float32)
    new_coef = flat_coef + summed
    return (new_cols, new_coef.reshape(members_here, tracers, -1))


def solution(mesh):
    in_specs = (
        P(("ens", "trc"), None, None, None),
        P(),
        P(),
        P(),
        P(),
        P(),
        P(),
        P("ens", None, None),
        P("trc", None),
        P("trc"),
        P("trc", None, None),
        P("trc", None, None),
        P(None, "trc", None, None),
    )
    out_specs = (P("ens", None, "trc", None), P("ens", None, None))
    return jax.shard_map(shards, mesh=mesh, in_specs=in_specs, out_specs=out_specs, check_vma=False)
```

```python
import jax
import jax.numpy as jnp
from jax import lax
from jax.sharding import PartitionSpec as P

OBS_TR = 6
ADV_STEPS = 2
OBS_CAP = 128


def transport(concentration, velocity, sea_mask):
    east_open = sea_mask * jnp.roll(sea_mask, -1, axis=1)
    north_open = sea_mask * jnp.concatenate([sea_mask[1:], jnp.zeros_like(sea_mask[:1])], axis=0)
    east_speed = velocity[0] * east_open
    north_speed = velocity[1] * north_open
    for _ in range(ADV_STEPS):
        east_value = jnp.roll(concentration, -1, axis=-1)
        east_flux = (
            jnp.maximum(east_speed, 0.0) * concentration + jnp.minimum(east_speed, 0.0) * east_value
        )
        north_value = jnp.concatenate(
            [concentration[..., 1:, :], jnp.zeros_like(concentration[..., :1, :])], axis=-2
        )
        north_flux = (
            jnp.maximum(north_speed, 0.0) * concentration
            + jnp.minimum(north_speed, 0.0) * north_value
        )
        west_flux = jnp.roll(east_flux, 1, axis=-1)
        south_flux = jnp.concatenate(
            [jnp.zeros_like(north_flux[..., :1, :]), north_flux[..., :-1, :]], axis=-2
        )
        concentration = concentration - (east_flux - west_flux) - (north_flux - south_flux)
    return concentration


def shift_lat(field, offset):
    zeros = jnp.zeros_like(field[..., :1, :])
    if offset > 0:
        return jnp.concatenate([field[..., 1:, :], zeros], axis=-2)
    return jnp.concatenate([zeros, field[..., :-1, :]], axis=-2)


def transport_stencil(concentration, velocity, sea_mask):
    east_open = sea_mask * jnp.roll(sea_mask, -1, axis=1)
    north_open = sea_mask * shift_lat(sea_mask, 1)
    east_speed = velocity[0] * east_open
    north_speed = velocity[1] * north_open
    east_out = jnp.maximum(east_speed, 0.0)
    east_in = jnp.minimum(east_speed, 0.0)
    north_out = jnp.maximum(north_speed, 0.0)
    north_in = jnp.minimum(north_speed, 0.0)
    west_out = jnp.roll(east_out, 1, axis=-1)
    west_in = jnp.roll(east_in, 1, axis=-1)
    south_out = shift_lat(north_out, -1)
    south_in = shift_lat(north_in, -1)
    centre = 1.0 - east_out + west_in - north_out + south_in
    for _ in range(ADV_STEPS):
        concentration = (
            centre * concentration
            - east_in * jnp.roll(concentration, -1, axis=-1)
            + west_out * jnp.roll(concentration, 1, axis=-1)
            - north_in * shift_lat(concentration, 1)
            + south_out * shift_lat(concentration, -1)
        )
    return concentration


def silu(value):
    return value * (0.5 + 0.5 * jnp.tanh(0.5 * value))


def tree_sum(value, axis_name, size):
    if size & (size - 1):
        return lax.psum(value, axis_name)
    step = 1
    while step < size:
        pairs = [(i, i ^ step) for i in range(size)]
        value = value + lax.ppermute(value, axis_name, pairs)
        step *= 2
    return value


def reaction(fields, in_weight, bias_one, hid_weight, bias_two, member_coef, sea_cells):
    contract = (((0,), (0,)), ((), ()))
    hidden_one = lax.dot_general(in_weight, fields, contract, preferred_element_type=jnp.float32)
    hidden_one = silu(hidden_one + bias_one[:, None]).astype(jnp.bfloat16)
    hidden_two = lax.dot_general(
        hid_weight, hidden_one, contract, preferred_element_type=jnp.float32
    )
    hidden_two = silu(hidden_two + bias_two[:, None]).astype(jnp.bfloat16)
    tendency = jnp.dot(
        member_coef, hidden_two, preferred_element_type=jnp.float32
    ) * hid_weight.shape[0] ** (-0.5)
    return ((fields.astype(jnp.float32) + tendency) * sea_cells).astype(jnp.bfloat16)


def solve_system(system, right_side):
    factor = jnp.linalg.cholesky(system)
    middle = lax.linalg.triangular_solve(factor, right_side, left_side=True, lower=True)
    return lax.linalg.triangular_solve(factor, middle, left_side=True, lower=True, transpose_a=True)


def shards(
    tracer_state,
    velocity,
    land_mask,
    in_weight,
    bias_one,
    hid_weight,
    bias_two,
    out_coef,
    obs_cell,
    obs_count,
    obs_value,
    obs_var,
    obs_noise,
):
    blocks = lax.axis_size("trc")
    own_block = lax.axis_index("trc")
    group_index = lax.axis_index("ens")
    field_rows, levels, lat_rows, lon_count = tracer_state.shape
    row_block = lat_rows // blocks
    block_width = row_block * lon_count
    members_here = out_coef.shape[0]
    tracers = in_weight.shape[0]
    group_rows = members_here * tracers
    highest = lax.Precision.HIGHEST
    sea_mask = land_mask.astype(jnp.float32)
    coef_all = lax.all_gather(out_coef.reshape(out_coef.shape[0], -1), "ens", axis=0, tiled=True)
    coef_half = out_coef.astype(jnp.bfloat16)
    sea_own = lax.dynamic_slice_in_dim(sea_mask, own_block * row_block, row_block, 0)
    sea_flat = sea_own.reshape(-1)
    scale = hid_weight.shape[0] ** (-0.5)
    level_cells = lax.broadcasted_iota(jnp.int32, (block_width, OBS_CAP), 0)
    picked = jnp.zeros((members_here * OBS_TR, OBS_CAP), jnp.float32)
    level_outs = []
    span = 2 if levels % 2 == 0 else 1
    for first in range(0, levels, span):
        state = tracer_state[:, first : first + span].astype(jnp.float32) * sea_mask
        advected = transport_stencil(state, velocity[:, first : first + span], sea_mask)
        advected = advected.astype(jnp.bfloat16)
        gathered = lax.all_to_all(advected, "trc", split_axis=2, concat_axis=0, tiled=True)
        fields = gathered.reshape(members_here, tracers, span, block_width)
        hidden_one = jnp.einsum(
            "tk,mtlc->mklc", in_weight, fields, preferred_element_type=jnp.float32
        )
        hidden_one = silu(hidden_one + bias_one[None, :, None, None]).astype(jnp.bfloat16)
        hidden_two = jnp.einsum(
            "jk,mjlc->mklc", hid_weight, hidden_one, preferred_element_type=jnp.float32
        )
        hidden_two = silu(hidden_two + bias_two[None, :, None, None]).astype(jnp.bfloat16)
        tendency = jnp.einsum(
            "mtk,mklc->mtlc", coef_half, hidden_two, preferred_element_type=jnp.float32
        ) * scale
        reacted = ((fields.astype(jnp.float32) + tendency) * sea_flat).astype(jnp.bfloat16)
        level_outs.append(reacted.reshape(group_rows, span, row_block, lon_count))
        for offset in range(span):
            observed = reacted[:, :OBS_TR, offset].reshape(members_here * OBS_TR, block_width)
            cell_base = (first + offset) * block_width
            picker = (level_cells + cell_base == obs_cell[0][None, :]).astype(jnp.bfloat16)
            picked = picked + jnp.dot(observed, picker, preferred_element_type=jnp.float32)
    new_cols = jnp.concatenate(level_outs, axis=1)
    predicted_own = picked.astype(jnp.bfloat16).reshape(members_here, OBS_TR, OBS_CAP)
    predicted_all = lax.all_gather(predicted_own, "ens", axis=0, tiled=True)
    member_total = predicted_all.shape[0]
    slot_ids = jnp.arange(OBS_CAP, dtype=jnp.int32)
    valid_slots = (slot_ids < obs_count[0]).astype(jnp.float32)
    weight = valid_slots[None, :] / obs_var[0]
    guessed = predicted_all.astype(jnp.float32).reshape(member_total, -1)
    anomaly = guessed - jnp.mean(guessed, axis=0)
    misfit = (obs_value[None] + obs_noise).reshape(member_total, -1) - guessed
    weighted = anomaly * weight.reshape(1, -1)
    gram_part = jnp.dot(weighted, anomaly.T, precision=highest, preferred_element_type=jnp.float32)
    cross_part = jnp.dot(weighted, misfit.T, precision=highest, preferred_element_type=jnp.float32)
    both = tree_sum(jnp.stack([gram_part, cross_part]), "trc", blocks)
    gram, cross = both[0], both[1]
    system = (member_total - 1) * jnp.eye(member_total, dtype=jnp.float32) + gram
    mixing = solve_system(system, cross)
    flat_coef = out_coef.reshape(members_here, -1)
    first_member = group_index * members_here
    mixing_cols = lax.dynamic_slice_in_dim(mixing, first_member, members_here, 1)
    summed = jnp.dot(mixing_cols.T, coef_all, precision=highest, preferred_element_type=jnp.float32)
    new_coef = flat_coef + summed
    return (new_cols, new_coef.reshape(members_here, tracers, -1))


def solution(mesh):
    in_specs = (
        P(("ens", "trc"), None, None, None),
        P(),
        P(),
        P(),
        P(),
        P(),
        P(),
        P("ens", None, None),
        P("trc", None),
        P("trc"),
        P("trc", None, None),
        P("trc", None, None),
        P(None, "trc", None, None),
    )
    out_specs = (P("ens", None, "trc", None), P("ens", None, None))
    return jax.shard_map(shards, mesh=mesh, in_specs=in_specs, out_specs=out_specs, check_vma=False)
```

```python
import functools

import jax
import jax.numpy as jnp
from jax import lax
from jax.experimental import pallas as pl
from jax.experimental.pallas import tpu as pltpu
from jax.sharding import PartitionSpec as P

OBS_TR = 6
ADV_STEPS = 2
OBS_CAP = 128


def transport(concentration, velocity, sea_mask):
    east_open = sea_mask * jnp.roll(sea_mask, -1, axis=1)
    north_open = sea_mask * jnp.concatenate([sea_mask[1:], jnp.zeros_like(sea_mask[:1])], axis=0)
    east_speed = velocity[0] * east_open
    north_speed = velocity[1] * north_open
    for _ in range(ADV_STEPS):
        east_value = jnp.roll(concentration, -1, axis=-1)
        east_flux = (
            jnp.maximum(east_speed, 0.0) * concentration + jnp.minimum(east_speed, 0.0) * east_value
        )
        north_value = jnp.concatenate(
            [concentration[..., 1:, :], jnp.zeros_like(concentration[..., :1, :])], axis=-2
        )
        north_flux = (
            jnp.maximum(north_speed, 0.0) * concentration
            + jnp.minimum(north_speed, 0.0) * north_value
        )
        west_flux = jnp.roll(east_flux, 1, axis=-1)
        south_flux = jnp.concatenate(
            [jnp.zeros_like(north_flux[..., :1, :]), north_flux[..., :-1, :]], axis=-2
        )
        concentration = concentration - (east_flux - west_flux) - (north_flux - south_flux)
    return concentration


def shift_lat(field, offset):
    zeros = jnp.zeros_like(field[..., :1, :])
    if offset > 0:
        return jnp.concatenate([field[..., 1:, :], zeros], axis=-2)
    return jnp.concatenate([zeros, field[..., :-1, :]], axis=-2)


def transport_stencil(concentration, velocity, sea_mask):
    east_open = sea_mask * jnp.roll(sea_mask, -1, axis=1)
    north_open = sea_mask * shift_lat(sea_mask, 1)
    east_speed = velocity[0] * east_open
    north_speed = velocity[1] * north_open
    east_out = jnp.maximum(east_speed, 0.0)
    east_in = jnp.minimum(east_speed, 0.0)
    north_out = jnp.maximum(north_speed, 0.0)
    north_in = jnp.minimum(north_speed, 0.0)
    west_out = jnp.roll(east_out, 1, axis=-1)
    west_in = jnp.roll(east_in, 1, axis=-1)
    south_out = shift_lat(north_out, -1)
    south_in = shift_lat(north_in, -1)
    centre = 1.0 - east_out + west_in - north_out + south_in
    for _ in range(ADV_STEPS):
        concentration = (
            centre * concentration
            - east_in * jnp.roll(concentration, -1, axis=-1)
            + west_out * jnp.roll(concentration, 1, axis=-1)
            - north_in * shift_lat(concentration, 1)
            + south_out * shift_lat(concentration, -1)
        )
    return concentration


def stencil_coefs(velocity, sea_mask):
    east_open = sea_mask * jnp.roll(sea_mask, -1, axis=1)
    north_open = sea_mask * shift_lat(sea_mask, 1)
    east_speed = velocity[0] * east_open
    north_speed = velocity[1] * north_open
    east_out = jnp.maximum(east_speed, 0.0)
    east_in = jnp.minimum(east_speed, 0.0)
    north_out = jnp.maximum(north_speed, 0.0)
    north_in = jnp.minimum(north_speed, 0.0)
    west_out = jnp.roll(east_out, 1, axis=-1)
    west_in = jnp.roll(east_in, 1, axis=-1)
    south_out = shift_lat(north_out, -1)
    south_in = shift_lat(north_in, -1)
    centre = 1.0 - east_out + west_in - north_out + south_in
    return jnp.stack([centre, -east_in, west_out, -north_in, south_out])

def advect_kernel(x_ref, sea_ref, coef_ref, o_ref, buf, *, steps, lon):
    width = buf.shape[-1]
    lats = buf.shape[-2]
    buf[...] = jnp.zeros(buf.shape, jnp.float32)
    buf[:, :, :lon] = x_ref[...].astype(jnp.float32) * sea_ref[...]
    conc = buf[...]
    lane = lax.broadcasted_iota(jnp.int32, conc.shape, 2)
    centre = coef_ref[0]
    east = coef_ref[1]
    west = coef_ref[2]
    north = coef_ref[3]
    south = coef_ref[4]
    for _ in range(steps):
        c_east = jnp.where(
            lane == lon - 1, pltpu.roll(conc, lon - 1, 2), pltpu.roll(conc, width - 1, 2)
        )
        c_west = jnp.where(lane == 0, pltpu.roll(conc, width - lon + 1, 2), pltpu.roll(conc, 1, 2))
        c_north = pltpu.roll(conc, lats - 1, 1)
        c_south = pltpu.roll(conc, 1, 1)
        conc = centre * conc + east * c_east + west * c_west + north * c_north + south * c_south
    o_ref[...] = conc[:, :, :lon].astype(o_ref.dtype)

def advect_level(tracer_state, level, coefs, sea_mask, steps, group=8):
    fields, _, lats, lon = tracer_state.shape
    width = ((lon + 127) // 128) * 128
    coefs = jnp.pad(coefs, ((0, 0), (0, 0), (0, width - lon)))
    kern = functools.partial(advect_kernel, steps=steps, lon=lon)
    return pl.pallas_call(
        kern,
        grid=(fields // group,),
        in_specs=[
            pl.BlockSpec((group, None, lats, lon), lambda g: (g, level, 0, 0)),
            pl.BlockSpec((lats, lon), lambda g: (0, 0)),
            pl.BlockSpec((5, lats, width), lambda g: (0, 0, 0)),
        ],
        out_specs=pl.BlockSpec((group, lats, lon), lambda g: (g, 0, 0)),
        out_shape=jax.ShapeDtypeStruct((fields, lats, lon), jnp.bfloat16),
        scratch_shapes=[pltpu.VMEM((group, lats, width), jnp.float32)],
    )(tracer_state, sea_mask, coefs)


def silu(value):
    return value * (0.5 + 0.5 * jnp.tanh(0.5 * value))


def tree_sum(value, axis_name, size):
    if size & (size - 1):
        return lax.psum(value, axis_name)
    step = 1
    while step < size:
        pairs = [(i, i ^ step) for i in range(size)]
        value = value + lax.ppermute(value, axis_name, pairs)
        step *= 2
    return value


def reaction(fields, in_weight, bias_one, hid_weight, bias_two, member_coef, sea_cells):
    contract = (((0,), (0,)), ((), ()))
    hidden_one = lax.dot_general(in_weight, fields, contract, preferred_element_type=jnp.float32)
    hidden_one = silu(hidden_one + bias_one[:, None]).astype(jnp.bfloat16)
    hidden_two = lax.dot_general(
        hid_weight, hidden_one, contract, preferred_element_type=jnp.float32
    )
    hidden_two = silu(hidden_two + bias_two[:, None]).astype(jnp.bfloat16)
    tendency = jnp.dot(
        member_coef, hidden_two, preferred_element_type=jnp.float32
    ) * hid_weight.shape[0] ** (-0.5)
    return ((fields.astype(jnp.float32) + tendency) * sea_cells).astype(jnp.bfloat16)


def solve_system(system, right_side):
    factor = jnp.linalg.cholesky(system)
    middle = lax.linalg.triangular_solve(factor, right_side, left_side=True, lower=True)
    return lax.linalg.triangular_solve(factor, middle, left_side=True, lower=True, transpose_a=True)


def shards(
    tracer_state,
    velocity,
    land_mask,
    in_weight,
    bias_one,
    hid_weight,
    bias_two,
    out_coef,
    obs_cell,
    obs_count,
    obs_value,
    obs_var,
    obs_noise,
):
    blocks = lax.axis_size("trc")
    own_block = lax.axis_index("trc")
    group_index = lax.axis_index("ens")
    field_rows, levels, lat_rows, lon_count = tracer_state.shape
    row_block = lat_rows // blocks
    block_width = row_block * lon_count
    members_here = out_coef.shape[0]
    tracers = in_weight.shape[0]
    group_rows = members_here * tracers
    highest = lax.Precision.HIGHEST
    sea_mask = land_mask.astype(jnp.float32)
    coef_all = lax.all_gather(out_coef.reshape(out_coef.shape[0], -1), "ens", axis=0, tiled=True)
    coef_half = out_coef.astype(jnp.bfloat16)
    sea_own = lax.dynamic_slice_in_dim(sea_mask, own_block * row_block, row_block, 0)
    sea_flat = sea_own.reshape(-1)
    scale = hid_weight.shape[0] ** (-0.5)
    level_cells = lax.broadcasted_iota(jnp.int32, (block_width, OBS_CAP), 0)
    picked = jnp.zeros((members_here * OBS_TR, OBS_CAP), jnp.float32)
    level_outs = []
    for level in range(levels):
        coefs = stencil_coefs(velocity[:, level], sea_mask)
        advected = advect_level(tracer_state, level, coefs, sea_mask, ADV_STEPS)
        gathered = lax.all_to_all(advected, "trc", split_axis=1, concat_axis=0, tiled=True)
        fields = gathered.reshape(members_here, tracers, block_width)
        hidden_one = jnp.einsum(
            "tk,mtc->mkc", in_weight, fields, preferred_element_type=jnp.float32
        )
        hidden_one = silu(hidden_one + bias_one[None, :, None]).astype(jnp.bfloat16)
        hidden_two = jnp.einsum(
            "jk,mjc->mkc", hid_weight, hidden_one, preferred_element_type=jnp.float32
        )
        hidden_two = silu(hidden_two + bias_two[None, :, None]).astype(jnp.bfloat16)
        tendency = jnp.einsum(
            "mtk,mkc->mtc", coef_half, hidden_two, preferred_element_type=jnp.float32
        ) * scale
        reacted = ((fields.astype(jnp.float32) + tendency) * sea_flat).astype(jnp.bfloat16)
        level_outs.append(reacted.reshape(group_rows, row_block, lon_count))
        observed = reacted[:, :OBS_TR].reshape(members_here * OBS_TR, block_width)
        picker = (level_cells + level * block_width == obs_cell[0][None, :]).astype(jnp.bfloat16)
        picked = picked + jnp.dot(observed, picker, preferred_element_type=jnp.float32)
    new_cols = jnp.stack(level_outs, axis=1)
    predicted_own = picked.astype(jnp.bfloat16).reshape(members_here, OBS_TR, OBS_CAP)
    predicted_all = lax.all_gather(predicted_own, "ens", axis=0, tiled=True)
    member_total = predicted_all.shape[0]
    slot_ids = jnp.arange(OBS_CAP, dtype=jnp.int32)
    valid_slots = (slot_ids < obs_count[0]).astype(jnp.float32)
    weight = valid_slots[None, :] / obs_var[0]
    guessed = predicted_all.astype(jnp.float32).reshape(member_total, -1)
    anomaly = guessed - jnp.mean(guessed, axis=0)
    misfit = (obs_value[None] + obs_noise).reshape(member_total, -1) - guessed
    weighted = anomaly * weight.reshape(1, -1)
    gram_part = jnp.dot(weighted, anomaly.T, precision=highest, preferred_element_type=jnp.float32)
    cross_part = jnp.dot(weighted, misfit.T, precision=highest, preferred_element_type=jnp.float32)
    both = tree_sum(jnp.stack([gram_part, cross_part]), "trc", blocks)
    gram, cross = both[0], both[1]
    system = (member_total - 1) * jnp.eye(member_total, dtype=jnp.float32) + gram
    mixing = solve_system(system, cross)
    flat_coef = out_coef.reshape(members_here, -1)
    first_member = group_index * members_here
    mixing_cols = lax.dynamic_slice_in_dim(mixing, first_member, members_here, 1)
    summed = jnp.dot(mixing_cols.T, coef_all, precision=highest, preferred_element_type=jnp.float32)
    new_coef = flat_coef + summed
    return (new_cols, new_coef.reshape(members_here, tracers, -1))


def solution(mesh):
    in_specs = (
        P(("ens", "trc"), None, None, None),
        P(),
        P(),
        P(),
        P(),
        P(),
        P(),
        P("ens", None, None),
        P("trc", None),
        P("trc"),
        P("trc", None, None),
        P("trc", None, None),
        P(None, "trc", None, None),
    )
    out_specs = (P("ens", None, "trc", None), P("ens", None, None))
    return jax.shard_map(shards, mesh=mesh, in_specs=in_specs, out_specs=out_specs, check_vma=False)
```

```python
import functools

import jax
import jax.numpy as jnp
from jax import lax
from jax.experimental import pallas as pl
from jax.experimental.pallas import tpu as pltpu
from jax.sharding import PartitionSpec as P

OBS_TR = 6
ADV_STEPS = 2
OBS_CAP = 128


def transport(concentration, velocity, sea_mask):
    east_open = sea_mask * jnp.roll(sea_mask, -1, axis=1)
    north_open = sea_mask * jnp.concatenate([sea_mask[1:], jnp.zeros_like(sea_mask[:1])], axis=0)
    east_speed = velocity[0] * east_open
    north_speed = velocity[1] * north_open
    for _ in range(ADV_STEPS):
        east_value = jnp.roll(concentration, -1, axis=-1)
        east_flux = (
            jnp.maximum(east_speed, 0.0) * concentration + jnp.minimum(east_speed, 0.0) * east_value
        )
        north_value = jnp.concatenate(
            [concentration[..., 1:, :], jnp.zeros_like(concentration[..., :1, :])], axis=-2
        )
        north_flux = (
            jnp.maximum(north_speed, 0.0) * concentration
            + jnp.minimum(north_speed, 0.0) * north_value
        )
        west_flux = jnp.roll(east_flux, 1, axis=-1)
        south_flux = jnp.concatenate(
            [jnp.zeros_like(north_flux[..., :1, :]), north_flux[..., :-1, :]], axis=-2
        )
        concentration = concentration - (east_flux - west_flux) - (north_flux - south_flux)
    return concentration


def shift_lat(field, offset):
    zeros = jnp.zeros_like(field[..., :1, :])
    if offset > 0:
        return jnp.concatenate([field[..., 1:, :], zeros], axis=-2)
    return jnp.concatenate([zeros, field[..., :-1, :]], axis=-2)


def transport_stencil(concentration, velocity, sea_mask):
    east_open = sea_mask * jnp.roll(sea_mask, -1, axis=1)
    north_open = sea_mask * shift_lat(sea_mask, 1)
    east_speed = velocity[0] * east_open
    north_speed = velocity[1] * north_open
    east_out = jnp.maximum(east_speed, 0.0)
    east_in = jnp.minimum(east_speed, 0.0)
    north_out = jnp.maximum(north_speed, 0.0)
    north_in = jnp.minimum(north_speed, 0.0)
    west_out = jnp.roll(east_out, 1, axis=-1)
    west_in = jnp.roll(east_in, 1, axis=-1)
    south_out = shift_lat(north_out, -1)
    south_in = shift_lat(north_in, -1)
    centre = 1.0 - east_out + west_in - north_out + south_in
    for _ in range(ADV_STEPS):
        concentration = (
            centre * concentration
            - east_in * jnp.roll(concentration, -1, axis=-1)
            + west_out * jnp.roll(concentration, 1, axis=-1)
            - north_in * shift_lat(concentration, 1)
            + south_out * shift_lat(concentration, -1)
        )
    return concentration


def stencil_coefs(velocity, sea_mask):
    east_open = sea_mask * jnp.roll(sea_mask, -1, axis=1)
    north_open = sea_mask * shift_lat(sea_mask, 1)
    east_speed = velocity[0] * east_open
    north_speed = velocity[1] * north_open
    east_out = jnp.maximum(east_speed, 0.0)
    east_in = jnp.minimum(east_speed, 0.0)
    north_out = jnp.maximum(north_speed, 0.0)
    north_in = jnp.minimum(north_speed, 0.0)
    west_out = jnp.roll(east_out, 1, axis=-1)
    west_in = jnp.roll(east_in, 1, axis=-1)
    south_out = shift_lat(north_out, -1)
    south_in = shift_lat(north_in, -1)
    centre = 1.0 - east_out + west_in - north_out + south_in
    return jnp.stack([centre, -east_in, west_out, -north_in, south_out])

def advect_kernel(x_ref, sea_ref, coef_ref, o_ref, buf, *, steps, lon):
    width = buf.shape[-1]
    lats = buf.shape[-2]
    buf[...] = jnp.zeros(buf.shape, jnp.float32)
    buf[:, :, :lon] = x_ref[...].astype(jnp.float32) * sea_ref[...]
    conc = buf[...]
    lane = lax.broadcasted_iota(jnp.int32, conc.shape, 2)
    centre = coef_ref[0]
    east = coef_ref[1]
    west = coef_ref[2]
    north = coef_ref[3]
    south = coef_ref[4]
    for _ in range(steps):
        c_east = jnp.where(
            lane == lon - 1, pltpu.roll(conc, lon - 1, 2), pltpu.roll(conc, width - 1, 2)
        )
        c_west = jnp.where(lane == 0, pltpu.roll(conc, width - lon + 1, 2), pltpu.roll(conc, 1, 2))
        c_north = pltpu.roll(conc, lats - 1, 1)
        c_south = pltpu.roll(conc, 1, 1)
        conc = centre * conc + east * c_east + west * c_west + north * c_north + south * c_south
    buf[...] = conc
    for row in range(lats):
        o_ref[row] = buf[:, row, :lon].astype(o_ref.dtype)

def advect_level(tracer_state, level, coefs, sea_mask, steps, group=8):
    fields, _, lats, lon = tracer_state.shape
    width = ((lon + 127) // 128) * 128
    coefs = jnp.pad(coefs, ((0, 0), (0, 0), (0, width - lon)))
    kern = functools.partial(advect_kernel, steps=steps, lon=lon)
    return pl.pallas_call(
        kern,
        grid=(fields // group,),
        in_specs=[
            pl.BlockSpec((group, None, lats, lon), lambda g: (g, level, 0, 0)),
            pl.BlockSpec((lats, lon), lambda g: (0, 0)),
            pl.BlockSpec((5, lats, width), lambda g: (0, 0, 0)),
        ],
        out_specs=pl.BlockSpec((lats, group, lon), lambda g: (0, g, 0)),
        out_shape=jax.ShapeDtypeStruct((lats, fields, lon), jnp.bfloat16),
        scratch_shapes=[pltpu.VMEM((group, lats, width), jnp.float32)],
    )(tracer_state, sea_mask, coefs)


def silu(value):
    return value * (0.5 + 0.5 * jnp.tanh(0.5 * value))


def tree_sum(value, axis_name, size):
    if size & (size - 1):
        return lax.psum(value, axis_name)
    step = 1
    while step < size:
        pairs = [(i, i ^ step) for i in range(size)]
        value = value + lax.ppermute(value, axis_name, pairs)
        step *= 2
    return value


def reaction(fields, in_weight, bias_one, hid_weight, bias_two, member_coef, sea_cells):
    contract = (((0,), (0,)), ((), ()))
    hidden_one = lax.dot_general(in_weight, fields, contract, preferred_element_type=jnp.float32)
    hidden_one = silu(hidden_one + bias_one[:, None]).astype(jnp.bfloat16)
    hidden_two = lax.dot_general(
        hid_weight, hidden_one, contract, preferred_element_type=jnp.float32
    )
    hidden_two = silu(hidden_two + bias_two[:, None]).astype(jnp.bfloat16)
    tendency = jnp.dot(
        member_coef, hidden_two, preferred_element_type=jnp.float32
    ) * hid_weight.shape[0] ** (-0.5)
    return ((fields.astype(jnp.float32) + tendency) * sea_cells).astype(jnp.bfloat16)


def solve_system(system, right_side):
    factor = jnp.linalg.cholesky(system)
    middle = lax.linalg.triangular_solve(factor, right_side, left_side=True, lower=True)
    return lax.linalg.triangular_solve(factor, middle, left_side=True, lower=True, transpose_a=True)


def shards(
    tracer_state,
    velocity,
    land_mask,
    in_weight,
    bias_one,
    hid_weight,
    bias_two,
    out_coef,
    obs_cell,
    obs_count,
    obs_value,
    obs_var,
    obs_noise,
):
    blocks = lax.axis_size("trc")
    own_block = lax.axis_index("trc")
    group_index = lax.axis_index("ens")
    field_rows, levels, lat_rows, lon_count = tracer_state.shape
    row_block = lat_rows // blocks
    block_width = row_block * lon_count
    members_here = out_coef.shape[0]
    tracers = in_weight.shape[0]
    group_rows = members_here * tracers
    highest = lax.Precision.HIGHEST
    sea_mask = land_mask.astype(jnp.float32)
    coef_all = lax.all_gather(out_coef.reshape(out_coef.shape[0], -1), "ens", axis=0, tiled=True)
    coef_half = out_coef.astype(jnp.bfloat16)
    sea_own = lax.dynamic_slice_in_dim(sea_mask, own_block * row_block, row_block, 0)
    sea_flat = sea_own.reshape(-1)
    scale = hid_weight.shape[0] ** (-0.5)
    level_cells = lax.broadcasted_iota(jnp.int32, (block_width, OBS_CAP), 0)
    picked = jnp.zeros((members_here * OBS_TR, OBS_CAP), jnp.float32)
    level_outs = []
    for level in range(levels):
        coefs = stencil_coefs(velocity[:, level], sea_mask)
        advected = advect_level(tracer_state, level, coefs, sea_mask, ADV_STEPS)
        gathered = lax.all_to_all(advected, "trc", split_axis=0, concat_axis=1, tiled=True)
        fields = gathered.transpose(1, 0, 2).reshape(members_here, tracers, block_width)
        hidden_one = jnp.einsum(
            "tk,mtc->mkc", in_weight, fields, preferred_element_type=jnp.float32
        )
        hidden_one = silu(hidden_one + bias_one[None, :, None]).astype(jnp.bfloat16)
        hidden_two = jnp.einsum(
            "jk,mjc->mkc", hid_weight, hidden_one, preferred_element_type=jnp.float32
        )
        hidden_two = silu(hidden_two + bias_two[None, :, None]).astype(jnp.bfloat16)
        tendency = jnp.einsum(
            "mtk,mkc->mtc", coef_half, hidden_two, preferred_element_type=jnp.float32
        ) * scale
        reacted = ((fields.astype(jnp.float32) + tendency) * sea_flat).astype(jnp.bfloat16)
        level_outs.append(reacted.reshape(group_rows, row_block, lon_count))
        observed = reacted[:, :OBS_TR].reshape(members_here * OBS_TR, block_width)
        picker = (level_cells + level * block_width == obs_cell[0][None, :]).astype(jnp.bfloat16)
        picked = picked + jnp.dot(observed, picker, preferred_element_type=jnp.float32)
    new_cols = jnp.stack(level_outs, axis=1)
    predicted_own = picked.astype(jnp.bfloat16).reshape(members_here, OBS_TR, OBS_CAP)
    predicted_all = lax.all_gather(predicted_own, "ens", axis=0, tiled=True)
    member_total = predicted_all.shape[0]
    slot_ids = jnp.arange(OBS_CAP, dtype=jnp.int32)
    valid_slots = (slot_ids < obs_count[0]).astype(jnp.float32)
    weight = valid_slots[None, :] / obs_var[0]
    guessed = predicted_all.astype(jnp.float32).reshape(member_total, -1)
    anomaly = guessed - jnp.mean(guessed, axis=0)
    misfit = (obs_value[None] + obs_noise).reshape(member_total, -1) - guessed
    weighted = anomaly * weight.reshape(1, -1)
    gram_part = jnp.dot(weighted, anomaly.T, precision=highest, preferred_element_type=jnp.float32)
    cross_part = jnp.dot(weighted, misfit.T, precision=highest, preferred_element_type=jnp.float32)
    both = tree_sum(jnp.stack([gram_part, cross_part]), "trc", blocks)
    gram, cross = both[0], both[1]
    system = (member_total - 1) * jnp.eye(member_total, dtype=jnp.float32) + gram
    mixing = solve_system(system, cross)
    flat_coef = out_coef.reshape(members_here, -1)
    first_member = group_index * members_here
    mixing_cols = lax.dynamic_slice_in_dim(mixing, first_member, members_here, 1)
    summed = jnp.dot(mixing_cols.T, coef_all, precision=highest, preferred_element_type=jnp.float32)
    new_coef = flat_coef + summed
    return (new_cols, new_coef.reshape(members_here, tracers, -1))


def solution(mesh):
    in_specs = (
        P(("ens", "trc"), None, None, None),
        P(),
        P(),
        P(),
        P(),
        P(),
        P(),
        P("ens", None, None),
        P("trc", None),
        P("trc"),
        P("trc", None, None),
        P("trc", None, None),
        P(None, "trc", None, None),
    )
    out_specs = (P("ens", None, "trc", None), P("ens", None, None))
    return jax.shard_map(shards, mesh=mesh, in_specs=in_specs, out_specs=out_specs, check_vma=False)
```

```python
import functools

import jax
import jax.numpy as jnp
from jax import lax
from jax.experimental import pallas as pl
from jax.experimental.pallas import tpu as pltpu
from jax.sharding import PartitionSpec as P

OBS_TR = 6
ADV_STEPS = 2
OBS_CAP = 128


def transport(concentration, velocity, sea_mask):
    east_open = sea_mask * jnp.roll(sea_mask, -1, axis=1)
    north_open = sea_mask * jnp.concatenate([sea_mask[1:], jnp.zeros_like(sea_mask[:1])], axis=0)
    east_speed = velocity[0] * east_open
    north_speed = velocity[1] * north_open
    for _ in range(ADV_STEPS):
        east_value = jnp.roll(concentration, -1, axis=-1)
        east_flux = (
            jnp.maximum(east_speed, 0.0) * concentration + jnp.minimum(east_speed, 0.0) * east_value
        )
        north_value = jnp.concatenate(
            [concentration[..., 1:, :], jnp.zeros_like(concentration[..., :1, :])], axis=-2
        )
        north_flux = (
            jnp.maximum(north_speed, 0.0) * concentration
            + jnp.minimum(north_speed, 0.0) * north_value
        )
        west_flux = jnp.roll(east_flux, 1, axis=-1)
        south_flux = jnp.concatenate(
            [jnp.zeros_like(north_flux[..., :1, :]), north_flux[..., :-1, :]], axis=-2
        )
        concentration = concentration - (east_flux - west_flux) - (north_flux - south_flux)
    return concentration


def shift_lat(field, offset):
    zeros = jnp.zeros_like(field[..., :1, :])
    if offset > 0:
        return jnp.concatenate([field[..., 1:, :], zeros], axis=-2)
    return jnp.concatenate([zeros, field[..., :-1, :]], axis=-2)


def transport_stencil(concentration, velocity, sea_mask):
    east_open = sea_mask * jnp.roll(sea_mask, -1, axis=1)
    north_open = sea_mask * shift_lat(sea_mask, 1)
    east_speed = velocity[0] * east_open
    north_speed = velocity[1] * north_open
    east_out = jnp.maximum(east_speed, 0.0)
    east_in = jnp.minimum(east_speed, 0.0)
    north_out = jnp.maximum(north_speed, 0.0)
    north_in = jnp.minimum(north_speed, 0.0)
    west_out = jnp.roll(east_out, 1, axis=-1)
    west_in = jnp.roll(east_in, 1, axis=-1)
    south_out = shift_lat(north_out, -1)
    south_in = shift_lat(north_in, -1)
    centre = 1.0 - east_out + west_in - north_out + south_in
    for _ in range(ADV_STEPS):
        concentration = (
            centre * concentration
            - east_in * jnp.roll(concentration, -1, axis=-1)
            + west_out * jnp.roll(concentration, 1, axis=-1)
            - north_in * shift_lat(concentration, 1)
            + south_out * shift_lat(concentration, -1)
        )
    return concentration


def stencil_coefs(velocity, sea_mask):
    east_open = sea_mask * jnp.roll(sea_mask, -1, axis=1)
    north_open = sea_mask * shift_lat(sea_mask, 1)
    east_speed = velocity[0] * east_open
    north_speed = velocity[1] * north_open
    east_out = jnp.maximum(east_speed, 0.0)
    east_in = jnp.minimum(east_speed, 0.0)
    north_out = jnp.maximum(north_speed, 0.0)
    north_in = jnp.minimum(north_speed, 0.0)
    west_out = jnp.roll(east_out, 1, axis=-1)
    west_in = jnp.roll(east_in, 1, axis=-1)
    south_out = shift_lat(north_out, -1)
    south_in = shift_lat(north_in, -1)
    centre = 1.0 - east_out + west_in - north_out + south_in
    return jnp.stack([centre, -east_in, west_out, -north_in, south_out])

def advect_kernel(x_ref, sea_ref, coef_ref, o_ref, buf, *, steps, lon):
    width = buf.shape[-1]
    lats = buf.shape[-2]
    buf[...] = jnp.zeros(buf.shape, jnp.float32)
    buf[:, :, :lon] = x_ref[...].astype(jnp.float32) * sea_ref[...]
    conc = buf[...]
    lane = lax.broadcasted_iota(jnp.int32, conc.shape, 2)
    centre = coef_ref[0]
    east = coef_ref[1]
    west = coef_ref[2]
    north = coef_ref[3]
    south = coef_ref[4]
    for _ in range(steps):
        c_east = jnp.where(
            lane == lon - 1, pltpu.roll(conc, lon - 1, 2), pltpu.roll(conc, width - 1, 2)
        )
        c_west = jnp.where(lane == 0, pltpu.roll(conc, width - lon + 1, 2), pltpu.roll(conc, 1, 2))
        c_north = pltpu.roll(conc, lats - 1, 1)
        c_south = pltpu.roll(conc, 1, 1)
        conc = centre * conc + east * c_east + west * c_west + north * c_north + south * c_south
    o_ref[...] = conc[:, :, :lon].astype(o_ref.dtype)

def advect_level(tracer_state, level, coefs, sea_mask, steps, group=8):
    fields, _, lats, lon = tracer_state.shape
    width = ((lon + 127) // 128) * 128
    coefs = jnp.pad(coefs, ((0, 0), (0, 0), (0, width - lon)))
    kern = functools.partial(advect_kernel, steps=steps, lon=lon)
    return pl.pallas_call(
        kern,
        grid=(fields // group,),
        in_specs=[
            pl.BlockSpec((group, None, lats, lon), lambda g: (g, level, 0, 0)),
            pl.BlockSpec((lats, lon), lambda g: (0, 0)),
            pl.BlockSpec((5, lats, width), lambda g: (0, 0, 0)),
        ],
        out_specs=pl.BlockSpec((group, lats, lon), lambda g: (g, 0, 0)),
        out_shape=jax.ShapeDtypeStruct((fields, lats, lon), jnp.bfloat16),
        scratch_shapes=[pltpu.VMEM((group, lats, width), jnp.float32)],
    )(tracer_state, sea_mask, coefs)


def silu(value):
    return value * (0.5 + 0.5 * jnp.tanh(0.5 * value))


def tree_sum(value, axis_name, size):
    if size & (size - 1):
        return lax.psum(value, axis_name)
    step = 1
    while step < size:
        pairs = [(i, i ^ step) for i in range(size)]
        value = value + lax.ppermute(value, axis_name, pairs)
        step *= 2
    return value


def reaction(fields, in_weight, bias_one, hid_weight, bias_two, member_coef, sea_cells):
    contract = (((0,), (0,)), ((), ()))
    hidden_one = lax.dot_general(in_weight, fields, contract, preferred_element_type=jnp.float32)
    hidden_one = silu(hidden_one + bias_one[:, None]).astype(jnp.bfloat16)
    hidden_two = lax.dot_general(
        hid_weight, hidden_one, contract, preferred_element_type=jnp.float32
    )
    hidden_two = silu(hidden_two + bias_two[:, None]).astype(jnp.bfloat16)
    tendency = jnp.dot(
        member_coef, hidden_two, preferred_element_type=jnp.float32
    ) * hid_weight.shape[0] ** (-0.5)
    return ((fields.astype(jnp.float32) + tendency) * sea_cells).astype(jnp.bfloat16)


def solve_system(system, right_side):
    factor = jnp.linalg.cholesky(system)
    middle = lax.linalg.triangular_solve(factor, right_side, left_side=True, lower=True)
    return lax.linalg.triangular_solve(factor, middle, left_side=True, lower=True, transpose_a=True)


def shards(
    tracer_state,
    velocity,
    land_mask,
    in_weight,
    bias_one,
    hid_weight,
    bias_two,
    out_coef,
    obs_cell,
    obs_count,
    obs_value,
    obs_var,
    obs_noise,
):
    blocks = lax.axis_size("trc")
    own_block = lax.axis_index("trc")
    group_index = lax.axis_index("ens")
    field_rows, levels, lat_rows, lon_count = tracer_state.shape
    row_block = lat_rows // blocks
    block_width = row_block * lon_count
    members_here = out_coef.shape[0]
    tracers = in_weight.shape[0]
    group_rows = members_here * tracers
    highest = lax.Precision.HIGHEST
    sea_mask = land_mask.astype(jnp.float32)
    coef_all = lax.all_gather(out_coef.reshape(out_coef.shape[0], -1), "ens", axis=0, tiled=True)
    coef_half = out_coef.astype(jnp.bfloat16)
    sea_own = lax.dynamic_slice_in_dim(sea_mask, own_block * row_block, row_block, 0)
    sea_flat = sea_own.reshape(-1)
    scale = hid_weight.shape[0] ** (-0.5)
    level_cells = lax.broadcasted_iota(jnp.int32, (block_width, OBS_CAP), 0)
    picked = jnp.zeros((members_here * OBS_TR, OBS_CAP), jnp.float32)
    level_outs = []
    span = 2 if levels % 2 == 0 else 1
    for first in range(0, levels, span):
        pieces = []
        for level in range(first, first + span):
            coefs = stencil_coefs(velocity[:, level], sea_mask)
            pieces.append(advect_level(tracer_state, level, coefs, sea_mask, ADV_STEPS))
        advected = jnp.stack(pieces, axis=1)
        exchanged = lax.all_to_all(advected, "trc", split_axis=2, concat_axis=0, tiled=True)
        for offset in range(span):
            level = first + offset
            fields = exchanged[:, offset].reshape(members_here, tracers, block_width)
            hidden_one = jnp.einsum(
                "tk,mtc->mkc", in_weight, fields, preferred_element_type=jnp.float32
            )
            hidden_one = silu(hidden_one + bias_one[None, :, None]).astype(jnp.bfloat16)
            hidden_two = jnp.einsum(
                "jk,mjc->mkc", hid_weight, hidden_one, preferred_element_type=jnp.float32
            )
            hidden_two = silu(hidden_two + bias_two[None, :, None]).astype(jnp.bfloat16)
            tendency = jnp.einsum(
                "mtk,mkc->mtc", coef_half, hidden_two, preferred_element_type=jnp.float32
            ) * scale
            reacted = ((fields.astype(jnp.float32) + tendency) * sea_flat).astype(jnp.bfloat16)
            level_outs.append(reacted.reshape(group_rows, row_block, lon_count))
            observed = reacted[:, :OBS_TR].reshape(members_here * OBS_TR, block_width)
            picker = (level_cells + level * block_width == obs_cell[0][None, :]).astype(jnp.bfloat16)
            picked = picked + jnp.dot(observed, picker, preferred_element_type=jnp.float32)
    new_cols = jnp.stack(level_outs, axis=1)
    predicted_own = picked.astype(jnp.bfloat16).reshape(members_here, OBS_TR, OBS_CAP)
    predicted_all = lax.all_gather(predicted_own, "ens", axis=0, tiled=True)
    member_total = predicted_all.shape[0]
    slot_ids = jnp.arange(OBS_CAP, dtype=jnp.int32)
    valid_slots = (slot_ids < obs_count[0]).astype(jnp.float32)
    weight = valid_slots[None, :] / obs_var[0]
    guessed = predicted_all.astype(jnp.float32).reshape(member_total, -1)
    anomaly = guessed - jnp.mean(guessed, axis=0)
    misfit = (obs_value[None] + obs_noise).reshape(member_total, -1) - guessed
    weighted = anomaly * weight.reshape(1, -1)
    gram_part = jnp.dot(weighted, anomaly.T, precision=highest, preferred_element_type=jnp.float32)
    cross_part = jnp.dot(weighted, misfit.T, precision=highest, preferred_element_type=jnp.float32)
    both = tree_sum(jnp.stack([gram_part, cross_part]), "trc", blocks)
    gram, cross = both[0], both[1]
    system = (member_total - 1) * jnp.eye(member_total, dtype=jnp.float32) + gram
    mixing = solve_system(system, cross)
    flat_coef = out_coef.reshape(members_here, -1)
    first_member = group_index * members_here
    mixing_cols = lax.dynamic_slice_in_dim(mixing, first_member, members_here, 1)
    summed = jnp.dot(mixing_cols.T, coef_all, precision=highest, preferred_element_type=jnp.float32)
    new_coef = flat_coef + summed
    return (new_cols, new_coef.reshape(members_here, tracers, -1))


def solution(mesh):
    in_specs = (
        P(("ens", "trc"), None, None, None),
        P(),
        P(),
        P(),
        P(),
        P(),
        P(),
        P("ens", None, None),
        P("trc", None),
        P("trc"),
        P("trc", None, None),
        P("trc", None, None),
        P(None, "trc", None, None),
    )
    out_specs = (P("ens", None, "trc", None), P("ens", None, None))
    return jax.shard_map(shards, mesh=mesh, in_specs=in_specs, out_specs=out_specs, check_vma=False)
```

```python
import functools

import jax
import jax.numpy as jnp
from jax import lax
from jax.experimental import pallas as pl
from jax.experimental.pallas import tpu as pltpu
from jax.sharding import PartitionSpec as P

OBS_TR = 6
ADV_STEPS = 2
OBS_CAP = 128


def transport(concentration, velocity, sea_mask):
    east_open = sea_mask * jnp.roll(sea_mask, -1, axis=1)
    north_open = sea_mask * jnp.concatenate([sea_mask[1:], jnp.zeros_like(sea_mask[:1])], axis=0)
    east_speed = velocity[0] * east_open
    north_speed = velocity[1] * north_open
    for _ in range(ADV_STEPS):
        east_value = jnp.roll(concentration, -1, axis=-1)
        east_flux = (
            jnp.maximum(east_speed, 0.0) * concentration + jnp.minimum(east_speed, 0.0) * east_value
        )
        north_value = jnp.concatenate(
            [concentration[..., 1:, :], jnp.zeros_like(concentration[..., :1, :])], axis=-2
        )
        north_flux = (
            jnp.maximum(north_speed, 0.0) * concentration
            + jnp.minimum(north_speed, 0.0) * north_value
        )
        west_flux = jnp.roll(east_flux, 1, axis=-1)
        south_flux = jnp.concatenate(
            [jnp.zeros_like(north_flux[..., :1, :]), north_flux[..., :-1, :]], axis=-2
        )
        concentration = concentration - (east_flux - west_flux) - (north_flux - south_flux)
    return concentration


def shift_lat(field, offset):
    zeros = jnp.zeros_like(field[..., :1, :])
    if offset > 0:
        return jnp.concatenate([field[..., 1:, :], zeros], axis=-2)
    return jnp.concatenate([zeros, field[..., :-1, :]], axis=-2)


def transport_stencil(concentration, velocity, sea_mask):
    east_open = sea_mask * jnp.roll(sea_mask, -1, axis=1)
    north_open = sea_mask * shift_lat(sea_mask, 1)
    east_speed = velocity[0] * east_open
    north_speed = velocity[1] * north_open
    east_out = jnp.maximum(east_speed, 0.0)
    east_in = jnp.minimum(east_speed, 0.0)
    north_out = jnp.maximum(north_speed, 0.0)
    north_in = jnp.minimum(north_speed, 0.0)
    west_out = jnp.roll(east_out, 1, axis=-1)
    west_in = jnp.roll(east_in, 1, axis=-1)
    south_out = shift_lat(north_out, -1)
    south_in = shift_lat(north_in, -1)
    centre = 1.0 - east_out + west_in - north_out + south_in
    for _ in range(ADV_STEPS):
        concentration = (
            centre * concentration
            - east_in * jnp.roll(concentration, -1, axis=-1)
            + west_out * jnp.roll(concentration, 1, axis=-1)
            - north_in * shift_lat(concentration, 1)
            + south_out * shift_lat(concentration, -1)
        )
    return concentration


def stencil_coefs(velocity, sea_mask):
    east_open = sea_mask * jnp.roll(sea_mask, -1, axis=1)
    north_open = sea_mask * shift_lat(sea_mask, 1)
    east_speed = velocity[0] * east_open
    north_speed = velocity[1] * north_open
    east_out = jnp.maximum(east_speed, 0.0)
    east_in = jnp.minimum(east_speed, 0.0)
    north_out = jnp.maximum(north_speed, 0.0)
    north_in = jnp.minimum(north_speed, 0.0)
    west_out = jnp.roll(east_out, 1, axis=-1)
    west_in = jnp.roll(east_in, 1, axis=-1)
    south_out = shift_lat(north_out, -1)
    south_in = shift_lat(north_in, -1)
    centre = 1.0 - east_out + west_in - north_out + south_in
    return jnp.stack([centre, -east_in, west_out, -north_in, south_out])

def advect_kernel(x_ref, sea_ref, coef_ref, o_ref, buf, *, steps, lon):
    width = buf.shape[-1]
    lats = buf.shape[-2]
    buf[...] = jnp.zeros(buf.shape, jnp.float32)
    buf[:, :, :lon] = x_ref[...].astype(jnp.float32) * sea_ref[...]
    conc = buf[...]
    lane = lax.broadcasted_iota(jnp.int32, conc.shape, 2)
    centre = coef_ref[0]
    east = coef_ref[1]
    west = coef_ref[2]
    north = coef_ref[3]
    south = coef_ref[4]
    for _ in range(steps):
        c_east = jnp.where(
            lane == lon - 1, pltpu.roll(conc, lon - 1, 2), pltpu.roll(conc, width - 1, 2)
        )
        c_west = jnp.where(lane == 0, pltpu.roll(conc, width - lon + 1, 2), pltpu.roll(conc, 1, 2))
        c_north = pltpu.roll(conc, lats - 1, 1)
        c_south = pltpu.roll(conc, 1, 1)
        conc = centre * conc + east * c_east + west * c_west + north * c_north + south * c_south
    o_ref[...] = conc[:, :, :lon].astype(o_ref.dtype)

def advect_level(tracer_state, level, coefs, sea_mask, steps, group=8):
    fields, _, lats, lon = tracer_state.shape
    width = ((lon + 127) // 128) * 128
    coefs = jnp.pad(coefs, ((0, 0), (0, 0), (0, width - lon)))
    kern = functools.partial(advect_kernel, steps=steps, lon=lon)
    return pl.pallas_call(
        kern,
        grid=(fields // group,),
        in_specs=[
            pl.BlockSpec((group, None, lats, lon), lambda g: (g, level, 0, 0)),
            pl.BlockSpec((lats, lon), lambda g: (0, 0)),
            pl.BlockSpec((5, lats, width), lambda g: (0, 0, 0)),
        ],
        out_specs=pl.BlockSpec((group, lats, lon), lambda g: (g, 0, 0)),
        out_shape=jax.ShapeDtypeStruct((fields, lats, lon), jnp.bfloat16),
        scratch_shapes=[pltpu.VMEM((group, lats, width), jnp.float32)],
    )(tracer_state, sea_mask, coefs)


def silu(value):
    return value * (0.5 + 0.5 * jnp.tanh(0.5 * value))


def tree_sum(value, axis_name, size):
    if size & (size - 1):
        return lax.psum(value, axis_name)
    step = 1
    while step < size:
        pairs = [(i, i ^ step) for i in range(size)]
        value = value + lax.ppermute(value, axis_name, pairs)
        step *= 2
    return value


def reaction(fields, in_weight, bias_one, hid_weight, bias_two, member_coef, sea_cells):
    contract = (((0,), (0,)), ((), ()))
    hidden_one = lax.dot_general(in_weight, fields, contract, preferred_element_type=jnp.float32)
    hidden_one = silu(hidden_one + bias_one[:, None]).astype(jnp.bfloat16)
    hidden_two = lax.dot_general(
        hid_weight, hidden_one, contract, preferred_element_type=jnp.float32
    )
    hidden_two = silu(hidden_two + bias_two[:, None]).astype(jnp.bfloat16)
    tendency = jnp.dot(
        member_coef, hidden_two, preferred_element_type=jnp.float32
    ) * hid_weight.shape[0] ** (-0.5)
    return ((fields.astype(jnp.float32) + tendency) * sea_cells).astype(jnp.bfloat16)


def solve_system(system, right_side):
    factor = jnp.linalg.cholesky(system)
    middle = lax.linalg.triangular_solve(factor, right_side, left_side=True, lower=True)
    return lax.linalg.triangular_solve(factor, middle, left_side=True, lower=True, transpose_a=True)


def shards(
    tracer_state,
    velocity,
    land_mask,
    in_weight,
    bias_one,
    hid_weight,
    bias_two,
    out_coef,
    obs_cell,
    obs_count,
    obs_value,
    obs_var,
    obs_noise,
):
    blocks = lax.axis_size("trc")
    own_block = lax.axis_index("trc")
    group_index = lax.axis_index("ens")
    field_rows, levels, lat_rows, lon_count = tracer_state.shape
    row_block = lat_rows // blocks
    block_width = row_block * lon_count
    members_here = out_coef.shape[0]
    tracers = in_weight.shape[0]
    group_rows = members_here * tracers
    highest = lax.Precision.HIGHEST
    sea_mask = land_mask.astype(jnp.float32)
    coef_all = lax.all_gather(out_coef.reshape(out_coef.shape[0], -1), "ens", axis=0, tiled=True)
    coef_half = out_coef.astype(jnp.bfloat16)
    sea_own = lax.dynamic_slice_in_dim(sea_mask, own_block * row_block, row_block, 0)
    sea_flat = sea_own.reshape(-1)
    scale = hid_weight.shape[0] ** (-0.5)
    level_cells = lax.broadcasted_iota(jnp.int32, (block_width, OBS_CAP), 0)
    picked = jnp.zeros((members_here * OBS_TR, OBS_CAP), jnp.float32)
    level_outs = []
    span = 2 if levels % 2 == 0 else 1
    for first in range(0, levels, span):
        pieces = []
        for level in range(first, first + span):
            coefs = stencil_coefs(velocity[:, level], sea_mask)
            pieces.append(advect_level(tracer_state, level, coefs, sea_mask, ADV_STEPS))
        advected = jnp.stack(pieces, axis=1)
        exchanged = lax.all_to_all(advected, "trc", split_axis=2, concat_axis=0, tiled=True)
        for offset in range(span):
            level = first + offset
            fields = exchanged[:, offset].reshape(members_here, tracers, block_width)
            hidden_one = jnp.einsum(
                "tk,mtc->mkc", in_weight, fields, preferred_element_type=jnp.float32
            )
            hidden_one = silu(hidden_one + bias_one[None, :, None]).astype(jnp.bfloat16)
            hidden_two = jnp.einsum(
                "jk,mjc->mkc", hid_weight, hidden_one, preferred_element_type=jnp.float32
            )
            hidden_two = silu(hidden_two + bias_two[None, :, None]).astype(jnp.bfloat16)
            tendency = jnp.einsum(
                "mtk,mkc->mtc", coef_half, hidden_two, preferred_element_type=jnp.float32
            ) * scale
            reacted = ((fields.astype(jnp.float32) + tendency) * sea_flat).astype(jnp.bfloat16)
            level_outs.append(reacted.reshape(group_rows, row_block, lon_count))
            observed = reacted[:, :OBS_TR].reshape(members_here * OBS_TR, block_width)
            picker = (level_cells + level * block_width == obs_cell[0][None, :]).astype(jnp.bfloat16)
            picked = picked + jnp.dot(observed, picker, preferred_element_type=jnp.float32)
    new_cols = jnp.stack(level_outs, axis=1)
    predicted_own = picked.astype(jnp.bfloat16).reshape(members_here, OBS_TR, OBS_CAP)
    predicted_all = lax.all_gather(predicted_own, "ens", axis=0, tiled=True)
    member_total = predicted_all.shape[0]
    slot_ids = jnp.arange(OBS_CAP, dtype=jnp.int32)
    valid_slots = (slot_ids < obs_count[0]).astype(jnp.float32)
    weight = valid_slots[None, :] / obs_var[0]
    guessed = predicted_all.astype(jnp.float32).reshape(member_total, -1)
    anomaly = guessed - jnp.mean(guessed, axis=0)
    misfit = (obs_value[None] + obs_noise).reshape(member_total, -1) - guessed
    weighted = anomaly * weight.reshape(1, -1)
    paired = jnp.concatenate([anomaly, misfit], axis=0)
    both_part = jnp.dot(weighted, paired.T, precision=highest, preferred_element_type=jnp.float32)
    both = tree_sum(both_part, "trc", blocks)
    gram, cross = both[:, :member_total], both[:, member_total:]
    system = (member_total - 1) * jnp.eye(member_total, dtype=jnp.float32) + gram
    mixing = solve_system(system, cross)
    flat_coef = out_coef.reshape(members_here, -1)
    first_member = group_index * members_here
    mixing_cols = lax.dynamic_slice_in_dim(mixing, first_member, members_here, 1)
    summed = jnp.dot(mixing_cols.T, coef_all, precision=highest, preferred_element_type=jnp.float32)
    new_coef = flat_coef + summed
    return (new_cols, new_coef.reshape(members_here, tracers, -1))


def solution(mesh):
    in_specs = (
        P(("ens", "trc"), None, None, None),
        P(),
        P(),
        P(),
        P(),
        P(),
        P(),
        P("ens", None, None),
        P("trc", None),
        P("trc"),
        P("trc", None, None),
        P("trc", None, None),
        P(None, "trc", None, None),
    )
    out_specs = (P("ens", None, "trc", None), P("ens", None, None))
    return jax.shard_map(shards, mesh=mesh, in_specs=in_specs, out_specs=out_specs, check_vma=False)
```
